32 devices in a mesh: seq: 8 (over z, y), exp: 4 (over x, core).
Axes of the slice: x: 2, y: 2, z: 4, core: 2. Of those that a mesh axis runs over, the one named last changes fastest.
Arguments:
- hidden: bfloat16 [4, 1024, 2048], P('exp', 'seq'), may hold values from -6 to 6
- lengths: int32 [4, 4], P('exp'), may hold values from 1 to 512, 1024 in all within a row
- attn_gain: float32 [2048], replicated, may hold values from 0 to 10
- w_qkv: bfloat16 [2048, 3, 16, 128], P(None, None, 'seq'), may hold values from -0.125 to 0.125
- w_out: bfloat16 [16, 128, 2048], P('seq'), may hold values from -0.125 to 0.125
- moe_gain: float32 [2048], replicated, may hold values from 0.5 to 1.5
- router: bfloat16 [2048, 16], replicated, may hold values from -8 to 8
- routes: int32 [4, 1024, 6], P('exp', 'seq'), may hold values from 0 to 15, all different within a row; in each aligned block of 128 rows (0 to 127, 128 to 255, ..., all dimensions but the last counted through in order) at most 56 rows name the same one
- w_gate_up: bfloat16 [32, 2, 704, 2048], P(('seq', 'exp')), may hold values from -0.125 to 0.125
- w_down: bfloat16 [32, 704, 2048], P(('seq', 'exp')), may hold values from -0.15625 to 0.15625
- final_gain: float32 [2048], replicated, may hold values from 0.5 to 1.5
- lm_head: bfloat16 [102400, 2048], P(('seq', 'exp')), may hold values from -4 to 4
Outputs:
- layer_out: bfloat16 [4, 1024, 2048], P('exp', 'seq')
- logprobs: float32 [16, 102400], P(None, ('seq', 'exp'))
The draws below stay inside these ranges and needn't reach their ends.
Inputs may be any that keep to these rules, and one draw needn't show every extreme that they name: `routes`: in the rows of one device no expert is named by more than 56 rows; in some devices one expert is named by exactly 56 rows. `lengths`: each row sums to 1024; its largest entry is 512.
All inputs are finite; a program needn't handle non-finite values.
Results may differ from the reference program's by a relative error of at most 0.0095.
The reference program's roundings to bfloat16 on the way count: a program that leaves them out, or rounds other values in their place, can miss the bound.
Values may be sent and summed in bfloat16 or wider, within the bound.
No kernel may reach another device: no remote copies, remote signals or barrier semaphores. Data moves between devices by JAX's collectives and lax.ppermute only.
A program may use at most 128 MiB of HBM per device.

```python
import math
import jax
import jax.numpy as jnp
import numpy as np
from jax import lax

D = 2048
HEADS = 16
HD = 128
MOE_FF = 1408
VOCAB = 102400
TOP = 6
SPLIT = 2
PROMPTS = 4
TOK_DEV = 128
SEQ_TOK = 1024
MOST_LEN = 512
EXPERTS = 16
FF_DEV = 704
CAP = 56
REQUESTS = 16
N_EXP = 4
DEVICES = 32


def draw_attn_gain(key, part):
    values = jax.random.uniform(key, (D,), jnp.float32, 0.5, 1.5)
    return values


def draw_router(key, part):
    first = jax.random.fold_in(jax.random.fold_in(key, 11), 0)
    normal_part = jax.random.truncated_normal(first, -4.0, 4.0, (D, EXPERTS), jnp.float32)
    values = normal_part * (0.5 / math.sqrt(D))
    return jnp.clip(values, -8.0, 8.0).astype(jnp.bfloat16)


def draw_lm_head(key, part):
    normal_part = jax.random.truncated_normal(jax.random.fold_in(key, 23), -4.0, 4.0, (VOCAB, D), jnp.float32)
    values = normal_part * (3.0 / math.sqrt(D))
    return jnp.clip(values, -4.0, 4.0).astype(jnp.bfloat16)


def steps_of(stream_key, shape, cuts, low, high):
    level, own = 1.0, jax.random.fold_in(stream_key, 6)
    for axis_at, parts in cuts:
        steps = jnp.exp(jax.random.uniform(jax.random.fold_in(own, axis_at), (parts,), jnp.float32, low / len(cuts), high / len(cuts)))
        level = level * jnp.repeat(steps, shape[axis_at] // parts).reshape([-1 if axis == axis_at else 1 for axis in range(len(shape))])
    return level


def profile(amount, total, reach, skew):
    loads = [(1 << 20) // math.isqrt(standing ** skew) + 1 for standing in range(2, amount + 1)]
    surplus, given = total - reach - (amount - 1), [1] * (amount - 1)
    while surplus > 0:
        candidates = [i for i in range(amount - 1) if given[i] < reach]
        pool, left = sum([loads[i] for i in candidates]), surplus
        for i in candidates:
            extra = min(reach - given[i], max(1, left * loads[i] // pool), surplus)
            given[i] = given[i] + extra
            surplus = surplus - extra
    return np.array([reach] + given)


def ragged_sizes(rng, number_of, total, limit, lean):
    if number_of == 2:
        one = jax.random.randint(rng, (), max(1, total - limit), min(limit, total - 1) + 1)
        return jnp.stack([one, total - one])
    tallies = jnp.asarray(profile(number_of, total, limit, lean), jnp.int32)
    couples = (number_of - 1) // 2
    giver, receiver = tallies[1:1 + 2 * couples:2], tallies[2:2 + 2 * couples:2]
    slack = jnp.minimum(giver - 1, limit - receiver)
    passed = jax.random.randint(jax.random.fold_in(rng, 1), (couples,), 0, 1 << 20) % (slack + 1)
    tallies = tallies.at[1:1 + 2 * couples:2].set(giver - passed).at[2:2 + 2 * couples:2].set(receiver + passed)
    return tallies[jax.random.permutation(jax.random.fold_in(rng, 2), number_of)]


def routed_block(own_key, own, number, rows, amount, top, most, lean):
    order = jax.random.permutation(own_key, amount)
    heavy_load, ordinary = shares(amount, rows * top, most, lean, True), shares(amount, rows * top, most, lean, False)
    places = jnp.arange(amount)

    def named(sizes, rotation):
        used = int((sizes > 0).sum())
        fixed = max(1, used // 4)
        shifted = fixed + (places - fixed + rotation * (used - fixed)) % max(1, amount - fixed)
        return jnp.zeros((amount,), jnp.int32).at[order[jnp.where(places < fixed, places, shifted)]].set(jnp.asarray(sizes, jnp.int32))

    sizes = jnp.where(number % 4 == 0, named(heavy_load, number // 4), named(ordinary, number - number // 4 - 1))
    mixed = jax.random.permutation(jax.random.fold_in(own, 3), amount)
    source_of, taker = mixed[0:amount // 2 * 2:2], mixed[1:amount // 2 * 2:2]
    room = jnp.minimum(sizes[source_of] - 1, most - sizes[taker]) // 2
    room = jnp.where((source_of == order[0]) | (taker == order[0]) | (sizes[taker] == 0), 0, jnp.maximum(room, 0))
    shifted = jax.random.randint(jax.random.fold_in(own, 4), (amount // 2,), 0, 1 << 20) % (room + 1)
    sizes = sizes.at[source_of].add(-shifted).at[taker].add(shifted)
    labels = jnp.searchsorted(jnp.cumsum(sizes), jnp.arange(rows * top), side="right").astype(jnp.int32)
    grid = labels.reshape(top, rows).T
    grid = grid[jax.random.permutation(jax.random.fold_in(own, 1), rows)]
    rotation = jax.random.randint(jax.random.fold_in(own, 2), (rows, 1), 0, top)
    return jnp.take_along_axis(grid, (jnp.arange(top)[None, :] + rotation) % top, axis=1)


def shares(count, total, limit, skew, full):
    portions = [(1 << 20) // math.isqrt(grade ** skew) + 1 for grade in range(1, count + 1)]
    largest = limit if full else min(limit, max(-(-total // count), total * portions[0] // sum(portions)))
    least = 1 if total - largest >= count - 1 else 0
    holding, surplus = [largest] + [least] * (count - 1), total - largest - least * (count - 1)
    while surplus > 0:
        candidates = [i for i in range(1, count) if holding[i] < largest] or [i for i in range(1, count) if holding[i] < limit]
        pool, left = sum([portions[i] for i in candidates]), surplus
        for i in candidates:
            more = min(limit - holding[i], max(1, left * portions[i] // pool), surplus)
            holding[i] = holding[i] + more
            surplus = surplus - more
    return np.array(holding)


def noise(rng, dims, scale, limit, pieces=(), held_as=jnp.bfloat16):
    array = scale * jax.random.normal(rng, dims, jnp.float32)
    if pieces:
        array = array * steps_of(rng, dims, pieces, -0.22, 0.18)
    return jnp.clip(array, -limit, limit).astype(held_as)


def setup_inputs(seed: int = 0) -> dict:
    arg_keys = jax.random.split(jax.random.key(seed), 13)
    hidden = noise(arg_keys[0], (N_EXP, SEQ_TOK, D), 1.0, 6.0, ((0, 4), (1, 8)))
    lengths = jax.vmap(lambda own: ragged_sizes(own, PROMPTS, SEQ_TOK, MOST_LEN, 2))(jax.random.split(arg_keys[1], N_EXP)).reshape((N_EXP, PROMPTS)).astype(jnp.int32)
    attn_gain = draw_attn_gain(jax.random.fold_in(arg_keys[12], 71), 0)
    w_qkv = noise(arg_keys[3], (D, 3, HEADS, HD), D ** -0.5, 0.125, ((2, 8),))
    w_out = noise(arg_keys[4], (HEADS, HD, D), (HEADS * HD) ** -0.5, 0.125, ((0, 8),))
    moe_gain = jnp.clip(1.0 + 0.1 * jax.random.normal(arg_keys[5], (D,), jnp.float32), 0.5, 1.5)
    router = draw_router(jax.random.fold_in(arg_keys[12], 71), 0)
    routes_keys = jax.random.split(jax.random.fold_in(arg_keys[7], 1), N_EXP * SEQ_TOK // TOK_DEV)
    routes_turns = jax.random.permutation(jax.random.fold_in(arg_keys[7], 3), N_EXP * SEQ_TOK // TOK_DEV)
    routes = jax.vmap(lambda own, number: routed_block(jax.random.fold_in(arg_keys[7], 2), own, number, TOK_DEV, EXPERTS, TOP, CAP, 1))(routes_keys, routes_turns).reshape((N_EXP, SEQ_TOK, TOP))
    w_gate_up = noise(arg_keys[8], (EXPERTS * SPLIT, 2, FF_DEV, D), D ** -0.5, 0.125, ((0, 32),))
    w_down = noise(arg_keys[9], (EXPERTS * SPLIT, FF_DEV, D), MOE_FF ** -0.5, 0.15625, ((0, 32),))
    final_gain = jnp.clip(1.0 + 0.1 * jax.random.normal(arg_keys[10], (D,), jnp.float32), 0.5, 1.5)
    lm_head = draw_lm_head(jax.random.fold_in(arg_keys[12], 71), 0)
    return {"hidden": hidden, "lengths": lengths, "attn_gain": attn_gain, "w_qkv": w_qkv, "w_out": w_out, "moe_gain": moe_gain, "router": router, "routes": routes, "w_gate_up": w_gate_up, "w_down": w_down, "final_gain": final_gain, "lm_head": lm_head}


epsilon = 1e-06

def rms_scale(values, gain):
    widened = values.astype(jnp.float32)
    inverse = lax.rsqrt(lax.optimization_barrier(jnp.mean(widened * widened, axis=-1, keepdims=True)) + epsilon)
    return widened * inverse * gain

def segment_layout(prompt_lengths, count):
    ends = jnp.cumsum(prompt_lengths).astype(jnp.int32)
    starts = (ends - prompt_lengths).astype(jnp.int32)
    places = jnp.arange(count, dtype=jnp.int32)
    member = ((places[:, None] >= starts[None, :]) & (places[:, None] < ends[None, :])).astype(jnp.int32)
    numbers = jnp.arange(prompt_lengths.shape[0], dtype=jnp.int32)
    segment = lax.optimization_barrier(jnp.sum(member * numbers[None, :], axis=1)).astype(jnp.int32)
    offset = (places - lax.optimization_barrier(jnp.sum(member * starts[None, :], axis=1))).astype(jnp.int32)
    return (segment, offset)

def rotary(values, positions):
    half_size = values.shape[-1] // 2
    freqs = 10000.0 ** (-2.0 * jnp.arange(half_size, dtype=jnp.float32) / values.shape[-1])
    angles = positions.astype(jnp.float32)[:, None] * freqs[None, :]
    cosine = jnp.cos(angles)[:, None, :]
    sine = jnp.sin(angles)[:, None, :]
    first_half = values[..., :half_size]
    second_half = values[..., half_size:]
    return jnp.concatenate([first_half * cosine - second_half * sine, second_half * cosine + first_half * sine], axis=-1)

def reference(hidden, lengths, attn_gain, w_qkv, w_out, moe_gain, router, routes, w_gate_up, w_down, final_gain, lm_head):
    scale_factor = HD ** (-0.5)
    qkv_weight = w_qkv.reshape(D, 3 * HEADS * HD)

    def attend(group):
        group_rows, prompt_lengths = group
        segment, offset = segment_layout(prompt_lengths, SEQ_TOK)
        normed = rms_scale(group_rows, attn_gain).astype(jnp.bfloat16)
        qkv = jnp.dot(normed, qkv_weight, preferred_element_type=jnp.float32).reshape(SEQ_TOK, 3, HEADS, HD)
        query = rotary(qkv[:, 0], offset).astype(jnp.bfloat16)
        keys = rotary(qkv[:, 1], offset).astype(jnp.bfloat16)
        values = qkv[:, 2].astype(jnp.bfloat16)
        scores = jnp.einsum('qhd,khd->hqk', query.astype(jnp.float32), keys.astype(jnp.float32)) * scale_factor
        places = jnp.arange(SEQ_TOK, dtype=jnp.int32)
        allowed = (segment[:, None] == segment[None, :]) & (places[None, :] <= places[:, None])
        scores = jnp.where(allowed[None], scores, -1e+30)
        highest = lax.optimization_barrier(jnp.max(scores, axis=2, keepdims=True))
        weights = jnp.exp(scores - highest)
        probs = (weights / lax.optimization_barrier(jnp.sum(weights, axis=2, keepdims=True))).astype(jnp.bfloat16)
        mixed_heads = jnp.einsum('hqk,khd->qhd', probs.astype(jnp.float32), values.astype(jnp.float32))
        return mixed_heads.astype(jnp.bfloat16).reshape(SEQ_TOK, HEADS * HD)
    heads = lax.map(attend, (hidden, lengths))
    token_count = N_EXP * SEQ_TOK
    flat_hidden = hidden.reshape(token_count, D)
    mix = jnp.dot(heads.reshape(token_count, HEADS * HD), w_out.reshape(HEADS * HD, D), preferred_element_type=jnp.float32)
    middle = (flat_hidden.astype(jnp.float32) + mix).astype(jnp.bfloat16)
    expert_in = rms_scale(middle, moe_gain).astype(jnp.bfloat16)
    logits = jnp.dot(expert_in, router, preferred_element_type=jnp.float32)
    flat_routes = routes.reshape(token_count, TOP)
    chosen = jnp.take_along_axis(logits, flat_routes, axis=1)
    gates = jax.nn.softmax(chosen, axis=-1)
    buffer_rows = CAP * DEVICES

    def expert_step(total, expert):
        hit = flat_routes == expert
        weight = lax.optimization_barrier(jnp.sum(jnp.where(hit, gates, 0.0), axis=1))
        marked = jnp.any(hit, axis=1)
        picked = jnp.nonzero(marked, size=buffer_rows, fill_value=0)[0].astype(jnp.int32)
        valid = (jnp.arange(buffer_rows, dtype=jnp.int32) < jnp.sum(marked.astype(jnp.int32))).astype(jnp.float32)
        chosen_rows = expert_in[picked]
        summed = jnp.zeros((buffer_rows, D), jnp.float32)
        for share in range(SPLIT):
            unit = (expert * SPLIT + share).astype(jnp.int32)
            pair = lax.dynamic_index_in_dim(w_gate_up, unit, 0, keepdims=False)
            down = lax.dynamic_index_in_dim(w_down, unit, 0, keepdims=False)
            gate_part = lax.dot_general(chosen_rows, pair[0], (((1,), (1,)), ((), ())), preferred_element_type=jnp.float32)
            up_part = lax.dot_general(chosen_rows, pair[1], (((1,), (1,)), ((), ())), preferred_element_type=jnp.float32)
            act = (jax.nn.silu(gate_part) * up_part).astype(jnp.bfloat16)
            part = jnp.dot(act, down, preferred_element_type=jnp.float32).astype(jnp.bfloat16)
            summed = summed + part.astype(jnp.float32)
        contrib = summed * (weight[picked] * valid)[:, None]
        return (total.at[picked].add(contrib), None)
    routed, _ = lax.scan(expert_step, jnp.zeros((token_count, D), jnp.float32), jnp.arange(EXPERTS, dtype=jnp.int32))
    layer_flat = (middle.astype(jnp.float32) + routed).astype(jnp.bfloat16)
    layer_out = layer_flat.reshape(N_EXP, SEQ_TOK, D)
    ends = jnp.cumsum(lengths, axis=1).astype(jnp.int32) - 1
    last = jnp.take_along_axis(layer_out, ends[:, :, None], axis=1).reshape(REQUESTS, D)
    final = rms_scale(last, final_gain).astype(jnp.bfloat16)
    vocab_scores = lax.dot_general(final, lm_head, (((1,), (1,)), ((), ())), preferred_element_type=jnp.float32)
    logprobs = vocab_scores - jax.nn.logsumexp(vocab_scores, axis=1, keepdims=True)
    return (layer_out, logprobs)
```

```python
import jax
import jax.numpy as jnp
from jax import lax
from jax.sharding import PartitionSpec as P

epsilon = 1e-06


def joined(value, axis, join):
    pieces = jax.tree.map(lambda part: lax.all_gather(part, axis), value)
    head = jax.tree.map(lambda part: part[0], pieces)
    tail = jax.tree.map(lambda part: part[1:], pieces)
    subtotal, _ = lax.scan(lambda subtotal, piece: (join(subtotal, piece), None), head, tail)
    return subtotal


def rms_scale(values, gain):
    widened = values.astype(jnp.float32)
    inverse = lax.rsqrt(jnp.mean(widened * widened, axis=-1, keepdims=True) + epsilon)
    return widened * inverse * gain


def segment_layout(prompt_lengths, count):
    ends = jnp.cumsum(prompt_lengths)
    starts = ends - prompt_lengths
    places = jnp.arange(count, dtype=jnp.int32)
    member = ((places[:, None] >= starts[None, :]) & (places[:, None] < ends[None, :])).astype(
        jnp.int32
    )
    numbers = jnp.arange(prompt_lengths.shape[0], dtype=jnp.int32)
    segment = jnp.sum(member * numbers[None, :], axis=1)
    offset = places - jnp.sum(member * starts[None, :], axis=1)
    return (segment, offset)


def rotary(values, positions):
    half_size = values.shape[-1] // 2
    freqs = 10000.0 ** (-2.0 * jnp.arange(half_size, dtype=jnp.float32) / values.shape[-1])
    angles = positions.astype(jnp.float32)[:, None] * freqs[None, :]
    cosine = jnp.cos(angles)[:, None, :]
    sine = jnp.sin(angles)[:, None, :]
    first_half = values[..., :half_size]
    second_half = values[..., half_size:]
    return jnp.concatenate(
        [first_half * cosine - second_half * sine, second_half * cosine + first_half * sine],
        axis=-1,
    )


def pair_swap(value):
    count = lax.axis_size("exp")
    return lax.ppermute(value, "exp", [(i, i ^ 1) for i in range(count)])


def merge_softmax(earlier, later):
    highest = jnp.maximum(earlier[0], later[0])
    return (
        highest,
        earlier[1] * jnp.exp(earlier[0] - highest) + later[1] * jnp.exp(later[0] - highest),
    )


def per_device(
    hidden,
    lengths,
    attn_gain,
    w_qkv,
    w_out,
    moe_gain,
    router,
    routes,
    w_gate_up,
    w_down,
    final_gain,
    lm_head,
):
    seq_count = lax.axis_size("seq")
    group_count = lax.axis_size("exp")
    device_count = seq_count * group_count
    token_rows = hidden[0]
    tok_rows = token_rows.shape[0]
    model_width = token_rows.shape[1]
    group_tokens = tok_rows * seq_count
    head_count = w_qkv.shape[2]
    head_size = w_qkv.shape[3]
    scale_factor = head_size ** (-0.5)
    prompt_lengths = lengths[0]
    segment, offset = segment_layout(prompt_lengths, group_tokens)
    normed = rms_scale(token_rows, attn_gain).astype(jnp.bfloat16)
    qkv_weight = w_qkv.reshape(model_width, 3 * head_count * head_size)
    qkv = jnp.dot(
        lax.all_gather(normed, "seq", axis=0, tiled=True),
        qkv_weight,
        preferred_element_type=jnp.float32,
    ).reshape(group_tokens, 3, head_count, head_size)
    query = rotary(qkv[:, 0], offset).astype(jnp.bfloat16)
    keys = rotary(qkv[:, 1], offset).astype(jnp.bfloat16)
    values = qkv[:, 2].astype(jnp.bfloat16)
    block_rows = min(512, group_tokens)
    key_places = jnp.arange(group_tokens, dtype=jnp.int32)

    def one_block(block_index):
        first_row = block_index * block_rows
        block_query = lax.dynamic_slice_in_dim(query, first_row, block_rows, 0)
        block_segment = lax.dynamic_slice_in_dim(segment, first_row, block_rows, 0)
        query_places = first_row + jnp.arange(block_rows, dtype=jnp.int32)
        scores = (
            jnp.einsum("qhd,khd->hqk", block_query, keys, preferred_element_type=jnp.float32)
            * scale_factor
        )
        allowed = (block_segment[:, None] == segment[None, :]) & (
            key_places[None, :] <= query_places[:, None]
        )
        scores = jnp.where(allowed[None], scores, -1e30)
        highest = jnp.max(scores, axis=2, keepdims=True)
        weights = jnp.exp(scores - highest)
        probs = (weights / jnp.sum(weights, axis=2, keepdims=True)).astype(jnp.bfloat16)
        return jnp.einsum("hqk,khd->qhd", probs, values, preferred_element_type=jnp.float32).astype(
            jnp.bfloat16
        )

    blocks = lax.map(one_block, jnp.arange(group_tokens // block_rows, dtype=jnp.int32))
    heads_flat = blocks.reshape(group_tokens, head_count * head_size)
    regrouped = lax.all_to_all(heads_flat, "seq", split_axis=0, concat_axis=1, tiled=True)
    core = lax.axis_index("exp") % 2
    half_size = head_size // 2
    own_half = lax.dynamic_slice_in_dim(w_out, core * half_size, half_size, axis=1)
    own_weight = lax.all_gather(own_half, "seq", axis=0, tiled=True)
    other_weight = pair_swap(own_weight)
    regrouped = regrouped.reshape(tok_rows, -1, head_size)
    own_heads = lax.dynamic_slice_in_dim(regrouped, core * half_size, half_size, axis=2)
    other_heads = lax.dynamic_slice_in_dim(regrouped, (1 - core) * half_size, half_size, axis=2)
    mixed = jnp.einsum(
        "thd,hdo->to", own_heads, own_weight, preferred_element_type=jnp.float32
    ) + jnp.einsum("thd,hdo->to", other_heads, other_weight, preferred_element_type=jnp.float32)
    middle = (token_rows.astype(jnp.float32) + mixed).astype(jnp.bfloat16)
    expert_in = rms_scale(middle, moe_gain).astype(jnp.bfloat16)
    logits = jnp.dot(expert_in, router, preferred_element_type=jnp.float32)
    expert_count = router.shape[1]
    token_routes = routes[0]
    top_count = token_routes.shape[1]
    expert_ids = jnp.arange(expert_count, dtype=jnp.int32)
    chosen_mask = token_routes[:, :, None] == expert_ids[None, None, :]
    chosen = jnp.sum(jnp.where(chosen_mask, logits[:, None, :], 0.0), axis=2)
    gates = jax.nn.softmax(chosen, axis=-1)
    capacity = max(2, tok_rows * top_count * 7 // (6 * expert_count))
    flat_mask = chosen_mask.reshape(tok_rows * top_count, expert_count).astype(jnp.int32)
    earlier_count = jnp.cumsum(flat_mask, axis=0) - flat_mask
    slot_index = jnp.sum(earlier_count * flat_mask, axis=1)
    target = (token_routes.reshape(-1) * capacity + slot_index).reshape(tok_rows, top_count)
    slot_total = expert_count * capacity
    placed = target[:, :, None] == jnp.arange(slot_total, dtype=jnp.int32)[None, None, :]
    dispatch_table = jnp.any(placed, axis=1).astype(jnp.bfloat16)
    slot_weights = jnp.sum(jnp.where(placed, gates[:, :, None], 0.0), axis=1)
    packed = lax.dot_general(
        dispatch_table, expert_in, (((0,), (0,)), ((), ())), preferred_element_type=jnp.float32
    ).astype(jnp.bfloat16)
    shares = device_count // expert_count
    assert capacity % shares == 0
    outgoing = packed.reshape(device_count, capacity // shares, model_width)
    gate_up = w_gate_up[0]
    down_weight = w_down[0]
    other_gate_up = pair_swap(gate_up)
    other_down = pair_swap(down_weight)
    arrived = lax.all_to_all(outgoing, ("seq", "exp"), split_axis=0, concat_axis=0, tiled=True)
    arrived_shape = arrived.shape
    flat_rows = arrived.reshape(-1, model_width)

    def share_part(pair, down):
        both = jnp.einsum("rd,gfd->rgf", flat_rows, pair, preferred_element_type=jnp.float32)
        act = (jax.nn.silu(both[:, 0]) * both[:, 1]).astype(jnp.bfloat16)
        part = jnp.dot(act, down, preferred_element_type=jnp.float32).astype(jnp.bfloat16)
        return part.astype(jnp.float32)

    part_sum = share_part(gate_up, down_weight) + share_part(other_gate_up, other_down)
    returned = lax.all_to_all(
        part_sum.astype(jnp.bfloat16).reshape(arrived_shape),
        ("seq", "exp"),
        split_axis=0,
        concat_axis=0,
        tiled=True,
    )
    summed = returned.reshape(slot_total, model_width).astype(jnp.float32)
    routed = jnp.dot(
        slot_weights, summed, precision=lax.Precision.HIGHEST, preferred_element_type=jnp.float32
    )
    layer_rows = (middle.astype(jnp.float32) + routed).astype(jnp.bfloat16)
    prompt_count = prompt_lengths.shape[0]
    last_places = jnp.cumsum(prompt_lengths) - 1
    here_places = lax.axis_index("seq") * tok_rows + jnp.arange(tok_rows, dtype=jnp.int32)
    select_table = (last_places[:, None] == here_places[None, :]).astype(jnp.bfloat16)
    picked = jnp.dot(select_table, layer_rows, preferred_element_type=jnp.float32)
    board = jnp.zeros((group_count * prompt_count, model_width), jnp.bfloat16)
    board = lax.dynamic_update_slice_in_dim(
        board, picked.astype(jnp.bfloat16), lax.axis_index("exp") * prompt_count, 0
    )
    last_rows = lax.psum(board, ("seq", "exp")).astype(jnp.float32)
    final = rms_scale(last_rows, final_gain).astype(jnp.bfloat16)
    vocab_scores = lax.dot_general(
        final, lm_head, (((1,), (1,)), ((), ())), preferred_element_type=jnp.float32
    )
    local_peak = jnp.max(vocab_scores, axis=1)
    local_total = jnp.sum(jnp.exp(vocab_scores - local_peak[:, None]), axis=1)
    global_peak, global_total = joined((local_peak, local_total), ("seq", "exp"), merge_softmax)
    logprobs = vocab_scores - (global_peak + jnp.log(global_total))[:, None]
    return (layer_rows[None], logprobs)


def solution(mesh):
    return jax.shard_map(
        per_device,
        mesh=mesh,
        in_specs=(
            P("exp", "seq", None),
            P("exp", None),
            P(),
            P(None, None, "seq", None),
            P("seq", None, None),
            P(),
            P(),
            P("exp", "seq", None),
            P(("seq", "exp"), None, None, None),
            P(("seq", "exp"), None, None),
            P(),
            P(("seq", "exp"), None),
        ),
        out_specs=(P("exp", "seq", None), P(None, ("seq", "exp"))),
        check_vma=False,
    )
```

```python
import jax
import jax.numpy as jnp
from jax import lax
from jax.sharding import PartitionSpec as P

epsilon = 1e-06


def joined(value, axis, join):
    pieces = jax.tree.map(lambda part: lax.all_gather(part, axis), value)
    head = jax.tree.map(lambda part: part[0], pieces)
    tail = jax.tree.map(lambda part: part[1:], pieces)
    subtotal, _ = lax.scan(lambda subtotal, piece: (join(subtotal, piece), None), head, tail)
    return subtotal


def rms_scale(values, gain):
    widened = values.astype(jnp.float32)
    inverse = lax.rsqrt(jnp.mean(widened * widened, axis=-1, keepdims=True) + epsilon)
    return widened * inverse * gain


def segment_layout(prompt_lengths, count):
    ends = jnp.cumsum(prompt_lengths)
    starts = ends - prompt_lengths
    places = jnp.arange(count, dtype=jnp.int32)
    member = ((places[:, None] >= starts[None, :]) & (places[:, None] < ends[None, :])).astype(
        jnp.int32
    )
    numbers = jnp.arange(prompt_lengths.shape[0], dtype=jnp.int32)
    segment = jnp.sum(member * numbers[None, :], axis=1)
    offset = places - jnp.sum(member * starts[None, :], axis=1)
    return (segment, offset)


def rotary(values, positions):
    half_size = values.shape[-1] // 2
    freqs = 10000.0 ** (-2.0 * jnp.arange(half_size, dtype=jnp.float32) / values.shape[-1])
    angles = positions.astype(jnp.float32)[:, None] * freqs[None, :]
    cosine = jnp.cos(angles)[:, None, :]
    sine = jnp.sin(angles)[:, None, :]
    first_half = values[..., :half_size]
    second_half = values[..., half_size:]
    return jnp.concatenate(
        [first_half * cosine - second_half * sine, second_half * cosine + first_half * sine],
        axis=-1,
    )


def pair_swap(value):
    count = lax.axis_size("exp")
    return lax.ppermute(value, "exp", [(i, i ^ 1) for i in range(count)])


def merge_softmax(earlier, later):
    highest = jnp.maximum(earlier[0], later[0])
    return (
        highest,
        earlier[1] * jnp.exp(earlier[0] - highest) + later[1] * jnp.exp(later[0] - highest),
    )


def per_device(
    hidden,
    lengths,
    attn_gain,
    w_qkv,
    w_out,
    moe_gain,
    router,
    routes,
    w_gate_up,
    w_down,
    final_gain,
    lm_head,
):
    seq_count = lax.axis_size("seq")
    group_count = lax.axis_size("exp")
    device_count = seq_count * group_count
    token_rows = hidden[0]
    tok_rows = token_rows.shape[0]
    model_width = token_rows.shape[1]
    group_tokens = tok_rows * seq_count
    head_count = w_qkv.shape[2]
    head_size = w_qkv.shape[3]
    scale_factor = head_size ** (-0.5)
    prompt_lengths = lengths[0]
    segment, offset = segment_layout(prompt_lengths, group_tokens)
    normed = rms_scale(token_rows, attn_gain).astype(jnp.bfloat16)
    qkv_weight = w_qkv.reshape(model_width, 3 * head_count * head_size)
    group_normed = lax.all_gather(normed, "seq", axis=0, tiled=True)
    core = lax.axis_index("exp") % 2
    half_size = head_size // 2
    own_half = lax.dynamic_slice_in_dim(w_out, core * half_size, half_size, axis=1)
    own_half, group_normed = lax.optimization_barrier((own_half, group_normed))
    own_weight = lax.all_gather(own_half, "seq", axis=0, tiled=True)
    qkv = jnp.dot(
        group_normed,
        qkv_weight,
        preferred_element_type=jnp.float32,
    ).reshape(group_tokens, 3, head_count, head_size)
    query = rotary(qkv[:, 0], offset).astype(jnp.bfloat16)
    keys = rotary(qkv[:, 1], offset).astype(jnp.bfloat16)
    values = qkv[:, 2].astype(jnp.bfloat16)
    block_count = 4
    block_rows = group_tokens // block_count
    key_places = jnp.arange(group_tokens, dtype=jnp.int32)

    def one_block(block_index):
        first_row = block_index * block_rows
        key_count = first_row + block_rows
        block_query = query[first_row:key_count]
        block_segment = segment[first_row:key_count]
        query_places = key_places[first_row:key_count]
        scores = (
            jnp.einsum(
                "qhd,khd->hqk", block_query, keys[:key_count], preferred_element_type=jnp.float32
            )
            * scale_factor
        )
        allowed = (block_segment[:, None] == segment[None, :key_count]) & (
            key_places[None, :key_count] <= query_places[:, None]
        )
        scores = jnp.where(allowed[None], scores, -1e30)
        highest = jnp.max(scores, axis=2, keepdims=True)
        weights = jnp.exp(scores - highest)
        probs = (weights / jnp.sum(weights, axis=2, keepdims=True)).astype(jnp.bfloat16)
        return jnp.einsum(
            "hqk,khd->qhd", probs, values[:key_count], preferred_element_type=jnp.float32
        ).astype(jnp.bfloat16)

    blocks = jnp.concatenate([one_block(index) for index in range(block_count)], axis=0)
    own_weight, blocks = lax.optimization_barrier((own_weight, blocks))
    heads_flat = blocks.reshape(group_tokens, head_count * head_size)
    regrouped = lax.all_to_all(heads_flat, "seq", split_axis=0, concat_axis=1, tiled=True)
    other_weight = pair_swap(own_weight)
    regrouped = regrouped.reshape(tok_rows, -1, head_size)
    own_heads = lax.dynamic_slice_in_dim(regrouped, core * half_size, half_size, axis=2)
    other_heads = lax.dynamic_slice_in_dim(regrouped, (1 - core) * half_size, half_size, axis=2)
    mixed = jnp.einsum(
        "thd,hdo->to", own_heads, own_weight, preferred_element_type=jnp.float32
    ) + jnp.einsum("thd,hdo->to", other_heads, other_weight, preferred_element_type=jnp.float32)
    middle = (token_rows.astype(jnp.float32) + mixed).astype(jnp.bfloat16)
    expert_in = rms_scale(middle, moe_gain).astype(jnp.bfloat16)
    logits = jnp.dot(expert_in, router, preferred_element_type=jnp.float32)
    expert_count = router.shape[1]
    token_routes = routes[0]
    top_count = token_routes.shape[1]
    expert_ids = jnp.arange(expert_count, dtype=jnp.int32)
    chosen_mask = token_routes[:, :, None] == expert_ids[None, None, :]
    chosen = jnp.sum(jnp.where(chosen_mask, logits[:, None, :], 0.0), axis=2)
    gates = jax.nn.softmax(chosen, axis=-1)
    capacity = max(2, tok_rows * top_count * 7 // (6 * expert_count))
    flat_mask = chosen_mask.reshape(tok_rows * top_count, expert_count).astype(jnp.int32)
    earlier_count = jnp.cumsum(flat_mask, axis=0) - flat_mask
    slot_index = jnp.sum(earlier_count * flat_mask, axis=1)
    target = (token_routes.reshape(-1) * capacity + slot_index).reshape(tok_rows, top_count)
    slot_total = expert_count * capacity
    placed = target[:, :, None] == jnp.arange(slot_total, dtype=jnp.int32)[None, None, :]
    shares = device_count // expert_count
    assert capacity % shares == 0
    per_dest = capacity // shares
    dispatch_table = jnp.any(placed, axis=1).astype(jnp.bfloat16)
    dispatch_table = dispatch_table.reshape(tok_rows, device_count, per_dest)
    slot_weights = jnp.sum(jnp.where(placed, gates[:, :, None], 0.0), axis=1)
    slot_weights = slot_weights.reshape(tok_rows, device_count, per_dest)
    outgoing = jnp.einsum(
        "tsc,tm->scm", dispatch_table, expert_in, preferred_element_type=jnp.float32
    ).astype(jnp.bfloat16)
    gate_up = w_gate_up[0]
    down_weight = w_down[0]
    other_gate_up = pair_swap(gate_up)
    other_down = pair_swap(down_weight)
    arrived = lax.all_to_all(outgoing, ("seq", "exp"), split_axis=0, concat_axis=0, tiled=True)

    def share_part(pair, down):
        both = jnp.einsum("scd,gfd->scgf", arrived, pair, preferred_element_type=jnp.float32)
        act = (jax.nn.silu(both[:, :, 0]) * both[:, :, 1]).astype(jnp.bfloat16)
        part = jnp.einsum("scf,fd->scd", act, down, preferred_element_type=jnp.float32)
        return part.astype(jnp.bfloat16).astype(jnp.float32)

    part_sum = share_part(gate_up, down_weight) + share_part(other_gate_up, other_down)
    returned = lax.all_to_all(
        part_sum.astype(jnp.bfloat16), ("seq", "exp"), split_axis=0, concat_axis=0, tiled=True
    )
    routed = jnp.einsum(
        "tsc,scm->tm",
        slot_weights,
        returned.astype(jnp.float32),
        precision=lax.Precision.HIGHEST,
        preferred_element_type=jnp.float32,
    )
    layer_rows = (middle.astype(jnp.float32) + routed).astype(jnp.bfloat16)
    prompt_count = prompt_lengths.shape[0]
    last_places = jnp.cumsum(prompt_lengths) - 1
    here_places = lax.axis_index("seq") * tok_rows + jnp.arange(tok_rows, dtype=jnp.int32)
    select_table = (last_places[:, None] == here_places[None, :]).astype(jnp.bfloat16)
    picked = jnp.dot(select_table, layer_rows, preferred_element_type=jnp.float32)
    outgoing_rows = jnp.broadcast_to(
        picked.astype(jnp.bfloat16)[None], (device_count, prompt_count, model_width)
    )
    arrived_rows = lax.all_to_all(
        outgoing_rows, ("seq", "exp"), split_axis=0, concat_axis=0, tiled=True
    ).astype(jnp.float32)
    last_rows = jnp.sum(
        arrived_rows.reshape(seq_count, group_count * prompt_count, model_width), axis=0
    )
    final = rms_scale(last_rows, final_gain).astype(jnp.bfloat16)
    vocab_scores = lax.dot_general(
        final, lm_head, (((1,), (1,)), ((), ())), preferred_element_type=jnp.float32
    )
    local_peak = jnp.max(vocab_scores, axis=1)
    local_total = jnp.sum(jnp.exp(vocab_scores - local_peak[:, None]), axis=1)
    local_stats = jnp.stack([local_peak, local_total])
    all_stats = lax.all_to_all(
        jnp.broadcast_to(local_stats[None], (device_count,) + local_stats.shape),
        ("seq", "exp"),
        split_axis=0,
        concat_axis=0,
        tiled=True,
    )
    all_peaks = all_stats[:, 0]
    global_peak = jnp.max(all_peaks, axis=0)
    global_total = jnp.sum(all_stats[:, 1] * jnp.exp(all_peaks - global_peak[None]), axis=0)
    logprobs = vocab_scores - (global_peak + jnp.log(global_total))[:, None]
    return (layer_rows[None], logprobs)


def solution(mesh):
    return jax.shard_map(
        per_device,
        mesh=mesh,
        in_specs=(
            P("exp", "seq", None),
            P("exp", None),
            P(),
            P(None, None, "seq", None),
            P("seq", None, None),
            P(),
            P(),
            P("exp", "seq", None),
            P(("seq", "exp"), None, None, None),
            P(("seq", "exp"), None, None),
            P(),
            P(("seq", "exp"), None),
        ),
        out_specs=(P("exp", "seq", None), P(None, ("seq", "exp"))),
        check_vma=False,
    )
```

```python
import jax
import jax.numpy as jnp
from jax import lax
from jax.sharding import PartitionSpec as P

epsilon = 1e-06


def joined(value, axis, join):
    pieces = jax.tree.map(lambda part: lax.all_gather(part, axis), value)
    head = jax.tree.map(lambda part: part[0], pieces)
    tail = jax.tree.map(lambda part: part[1:], pieces)
    subtotal, _ = lax.scan(lambda subtotal, piece: (join(subtotal, piece), None), head, tail)
    return subtotal


def rms_scale(values, gain):
    widened = values.astype(jnp.float32)
    inverse = lax.rsqrt(jnp.mean(widened * widened, axis=-1, keepdims=True) + epsilon)
    return widened * inverse * gain


def segment_layout(prompt_lengths, count):
    ends = jnp.cumsum(prompt_lengths)
    starts = ends - prompt_lengths
    places = jnp.arange(count, dtype=jnp.int32)
    member = ((places[:, None] >= starts[None, :]) & (places[:, None] < ends[None, :])).astype(
        jnp.int32
    )
    numbers = jnp.arange(prompt_lengths.shape[0], dtype=jnp.int32)
    segment = jnp.sum(member * numbers[None, :], axis=1)
    offset = places - jnp.sum(member * starts[None, :], axis=1)
    return (segment, offset)


def rotary(values, positions):
    half_size = values.shape[-1] // 2
    freqs = 10000.0 ** (-2.0 * jnp.arange(half_size, dtype=jnp.float32) / values.shape[-1])
    angles = positions.astype(jnp.float32)[:, None] * freqs[None, :]
    cosine = jnp.cos(angles)[:, None, :]
    sine = jnp.sin(angles)[:, None, :]
    first_half = values[..., :half_size]
    second_half = values[..., half_size:]
    return jnp.concatenate(
        [first_half * cosine - second_half * sine, second_half * cosine + first_half * sine],
        axis=-1,
    )


def pair_swap(value):
    count = lax.axis_size("exp")
    return lax.ppermute(value, "exp", [(i, i ^ 1) for i in range(count)])


def merge_softmax(earlier, later):
    highest = jnp.maximum(earlier[0], later[0])
    return (
        highest,
        earlier[1] * jnp.exp(earlier[0] - highest) + later[1] * jnp.exp(later[0] - highest),
    )


def per_device(
    hidden,
    lengths,
    attn_gain,
    w_qkv,
    w_out,
    moe_gain,
    router,
    routes,
    w_gate_up,
    w_down,
    final_gain,
    lm_head,
):
    seq_count = lax.axis_size("seq")
    group_count = lax.axis_size("exp")
    device_count = seq_count * group_count
    token_rows = hidden[0]
    tok_rows = token_rows.shape[0]
    model_width = token_rows.shape[1]
    group_tokens = tok_rows * seq_count
    head_count = w_qkv.shape[2]
    head_size = w_qkv.shape[3]
    scale_factor = head_size ** (-0.5)
    prompt_lengths = lengths[0]
    segment, offset = segment_layout(prompt_lengths, group_tokens)
    normed = rms_scale(token_rows, attn_gain).astype(jnp.bfloat16)
    group_normed = lax.all_gather(normed, "seq", axis=0, tiled=True)
    core = lax.axis_index("exp") % 2
    half_size = head_size // 2
    own_half = lax.dynamic_slice_in_dim(w_out, core * half_size, half_size, axis=1)
    own_weight = lax.all_to_all(
        jnp.broadcast_to(own_half[None], (seq_count,) + own_half.shape),
        "seq",
        split_axis=0,
        concat_axis=0,
        tiled=True,
    ).reshape((-1,) + own_half.shape[1:])
    qkv = jnp.einsum("td,dshe->tshe", group_normed, w_qkv, preferred_element_type=jnp.float32)
    query = rotary(qkv[:, 0], offset).astype(jnp.bfloat16)
    keys = rotary(qkv[:, 1], offset).astype(jnp.bfloat16)
    values = qkv[:, 2].astype(jnp.bfloat16)
    block_count = 4
    block_rows = group_tokens // block_count
    key_places = jnp.arange(group_tokens, dtype=jnp.int32)

    def one_block(block_index):
        first_row = block_index * block_rows
        key_count = first_row + block_rows
        block_query = query[first_row:key_count]
        block_segment = segment[first_row:key_count]
        query_places = key_places[first_row:key_count]
        scores = (
            jnp.einsum(
                "qhd,khd->hqk", block_query, keys[:key_count], preferred_element_type=jnp.float32
            )
            * scale_factor
        )
        allowed = (block_segment[:, None] == segment[None, :key_count]) & (
            key_places[None, :key_count] <= query_places[:, None]
        )
        scores = jnp.where(allowed[None], scores, -1e30)
        highest = jnp.max(scores, axis=2, keepdims=True)
        weights = jnp.exp(scores - highest)
        probs = (weights / jnp.sum(weights, axis=2, keepdims=True)).astype(jnp.bfloat16)
        return jnp.einsum(
            "hqk,khd->qhd", probs, values[:key_count], preferred_element_type=jnp.float32
        ).astype(jnp.bfloat16)

    blocks = jnp.concatenate([one_block(index) for index in range(block_count)], axis=0)
    own_weight, blocks = lax.optimization_barrier((own_weight, blocks))
    heads_flat = blocks.reshape(group_tokens, head_count * head_size)
    regrouped = lax.all_to_all(heads_flat, "seq", split_axis=0, concat_axis=1, tiled=True)
    other_weight = pair_swap(own_weight)
    regrouped = regrouped.reshape(tok_rows, -1, head_size)
    own_heads = lax.dynamic_slice_in_dim(regrouped, core * half_size, half_size, axis=2)
    other_heads = lax.dynamic_slice_in_dim(regrouped, (1 - core) * half_size, half_size, axis=2)
    mixed = jnp.einsum(
        "thd,hdo->to", own_heads, own_weight, preferred_element_type=jnp.float32
    ) + jnp.einsum("thd,hdo->to", other_heads, other_weight, preferred_element_type=jnp.float32)
    middle = (token_rows.astype(jnp.float32) + mixed).astype(jnp.bfloat16)
    expert_in = rms_scale(middle, moe_gain).astype(jnp.bfloat16)
    logits = jnp.dot(expert_in, router, preferred_element_type=jnp.float32)
    expert_count = router.shape[1]
    token_routes = routes[0]
    top_count = token_routes.shape[1]
    expert_ids = jnp.arange(expert_count, dtype=jnp.int32)
    chosen_mask = token_routes[:, :, None] == expert_ids[None, None, :]
    chosen = jnp.sum(jnp.where(chosen_mask, logits[:, None, :], 0.0), axis=2)
    gates = jax.nn.softmax(chosen, axis=-1)
    capacity = max(2, tok_rows * top_count * 7 // (6 * expert_count))
    flat_mask = chosen_mask.reshape(tok_rows * top_count, expert_count).astype(jnp.int32)
    earlier_count = jnp.cumsum(flat_mask, axis=0) - flat_mask
    slot_index = jnp.sum(earlier_count * flat_mask, axis=1)
    target = (token_routes.reshape(-1) * capacity + slot_index).reshape(tok_rows, top_count)
    slot_total = expert_count * capacity
    placed = target[:, :, None] == jnp.arange(slot_total, dtype=jnp.int32)[None, None, :]
    shares = device_count // expert_count
    assert capacity % shares == 0
    per_dest = capacity // shares
    dispatch_table = jnp.any(placed, axis=1).astype(jnp.bfloat16)
    dispatch_table = dispatch_table.reshape(tok_rows, device_count, per_dest)
    slot_weights = jnp.sum(jnp.where(placed, gates[:, :, None], 0.0), axis=1)
    slot_weights = slot_weights.reshape(tok_rows, device_count, per_dest)
    outgoing = jnp.einsum(
        "tsc,tm->scm", dispatch_table, expert_in, preferred_element_type=jnp.float32
    ).astype(jnp.bfloat16)
    gate_up = w_gate_up[0]
    down_weight = w_down[0]
    other_gate_up = pair_swap(gate_up)
    other_down = pair_swap(down_weight)
    arrived = lax.all_to_all(outgoing, ("seq", "exp"), split_axis=0, concat_axis=0, tiled=True)

    def share_part(pair, down):
        both = jnp.einsum("scd,gfd->scgf", arrived, pair, preferred_element_type=jnp.float32)
        act = (jax.nn.silu(both[:, :, 0]) * both[:, :, 1]).astype(jnp.bfloat16)
        part = jnp.einsum("scf,fd->scd", act, down, preferred_element_type=jnp.float32)
        return part.astype(jnp.bfloat16).astype(jnp.float32)

    part_sum = share_part(gate_up, down_weight) + share_part(other_gate_up, other_down)
    returned = lax.all_to_all(
        part_sum.astype(jnp.bfloat16), ("seq", "exp"), split_axis=0, concat_axis=0, tiled=True
    )
    routed = jnp.einsum(
        "tsc,scm->tm",
        slot_weights,
        returned.astype(jnp.float32),
        precision=lax.Precision.HIGHEST,
        preferred_element_type=jnp.float32,
    )
    layer_rows = (middle.astype(jnp.float32) + routed).astype(jnp.bfloat16)
    prompt_count = prompt_lengths.shape[0]
    last_places = jnp.cumsum(prompt_lengths) - 1
    here_places = lax.axis_index("seq") * tok_rows + jnp.arange(tok_rows, dtype=jnp.int32)
    select_table = (last_places[:, None] == here_places[None, :]).astype(jnp.bfloat16)
    picked = jnp.dot(select_table, layer_rows, preferred_element_type=jnp.float32)
    outgoing_rows = jnp.broadcast_to(
        picked.astype(jnp.bfloat16)[None], (device_count, prompt_count, model_width)
    )
    arrived_rows = lax.all_to_all(
        outgoing_rows, ("seq", "exp"), split_axis=0, concat_axis=0, tiled=True
    ).astype(jnp.float32)
    last_rows = jnp.sum(
        arrived_rows.reshape(seq_count, group_count * prompt_count, model_width), axis=0
    )
    final = rms_scale(last_rows, final_gain).astype(jnp.bfloat16)
    vocab_scores = lax.dot_general(
        final, lm_head, (((1,), (1,)), ((), ())), preferred_element_type=jnp.float32
    )
    local_peak = jnp.max(vocab_scores, axis=1)
    local_total = jnp.sum(jnp.exp(vocab_scores - local_peak[:, None]), axis=1)
    local_stats = jnp.stack([local_peak, local_total])
    all_stats = lax.all_to_all(
        jnp.broadcast_to(local_stats[None], (device_count,) + local_stats.shape),
        ("seq", "exp"),
        split_axis=0,
        concat_axis=0,
        tiled=True,
    )
    all_peaks = all_stats[:, 0]
    global_peak = jnp.max(all_peaks, axis=0)
    global_total = jnp.sum(all_stats[:, 1] * jnp.exp(all_peaks - global_peak[None]), axis=0)
    logprobs = vocab_scores - (global_peak + jnp.log(global_total))[:, None]
    return (layer_rows[None], logprobs)


def solution(mesh):
    return jax.shard_map(
        per_device,
        mesh=mesh,
        in_specs=(
            P("exp", "seq", None),
            P("exp", None),
            P(),
            P(None, None, "seq", None),
            P("seq", None, None),
            P(),
            P(),
            P("exp", "seq", None),
            P(("seq", "exp"), None, None, None),
            P(("seq", "exp"), None, None),
            P(),
            P(("seq", "exp"), None),
        ),
        out_specs=(P("exp", "seq", None), P(None, ("seq", "exp"))),
        check_vma=False,
    )
```

```python
import jax
import jax.numpy as jnp
from jax import lax
from jax.sharding import PartitionSpec as P

epsilon = 1e-06


def joined(value, axis, join):
    pieces = jax.tree.map(lambda part: lax.all_gather(part, axis), value)
    head = jax.tree.map(lambda part: part[0], pieces)
    tail = jax.tree.map(lambda part: part[1:], pieces)
    subtotal, _ = lax.scan(lambda subtotal, piece: (join(subtotal, piece), None), head, tail)
    return subtotal


def rms_scale(values, gain):
    widened = values.astype(jnp.float32)
    inverse = lax.rsqrt(jnp.mean(widened * widened, axis=-1, keepdims=True) + epsilon)
    return widened * inverse * gain


def segment_layout(prompt_lengths, count):
    ends = jnp.cumsum(prompt_lengths)
    starts = ends - prompt_lengths
    places = jnp.arange(count, dtype=jnp.int32)
    member = ((places[:, None] >= starts[None, :]) & (places[:, None] < ends[None, :])).astype(
        jnp.int32
    )
    numbers = jnp.arange(prompt_lengths.shape[0], dtype=jnp.int32)
    segment = jnp.sum(member * numbers[None, :], axis=1)
    offset = places - jnp.sum(member * starts[None, :], axis=1)
    return (segment, offset)


def rotary(values, positions):
    half_size = values.shape[-1] // 2
    freqs = 10000.0 ** (-2.0 * jnp.arange(half_size, dtype=jnp.float32) / values.shape[-1])
    angles = positions.astype(jnp.float32)[:, None] * freqs[None, :]
    cosine = jnp.cos(angles)[:, None, :]
    sine = jnp.sin(angles)[:, None, :]
    first_half = values[..., :half_size]
    second_half = values[..., half_size:]
    return jnp.concatenate(
        [first_half * cosine - second_half * sine, second_half * cosine + first_half * sine],
        axis=-1,
    )


def pair_swap(value):
    count = lax.axis_size("exp")
    return lax.ppermute(value, "exp", [(i, i ^ 1) for i in range(count)])


def merge_softmax(earlier, later):
    highest = jnp.maximum(earlier[0], later[0])
    return (
        highest,
        earlier[1] * jnp.exp(earlier[0] - highest) + later[1] * jnp.exp(later[0] - highest),
    )


def per_device(
    hidden,
    lengths,
    attn_gain,
    w_qkv,
    w_out,
    moe_gain,
    router,
    routes,
    w_gate_up,
    w_down,
    final_gain,
    lm_head,
):
    seq_count = lax.axis_size("seq")
    group_count = lax.axis_size("exp")
    device_count = seq_count * group_count
    token_rows = hidden[0]
    tok_rows = token_rows.shape[0]
    model_width = token_rows.shape[1]
    group_tokens = tok_rows * seq_count
    head_count = w_qkv.shape[2]
    head_size = w_qkv.shape[3]
    scale_factor = head_size ** (-0.5)
    prompt_lengths = lengths[0]
    segment, offset = segment_layout(prompt_lengths, group_tokens)
    normed = rms_scale(token_rows, attn_gain).astype(jnp.bfloat16)
    group_normed = lax.all_gather(normed, "seq", axis=0, tiled=True)
    core = lax.axis_index("exp") % 2
    half_size = head_size // 2
    own_half = lax.dynamic_slice_in_dim(w_out, core * half_size, half_size, axis=1)
    own_weight = lax.all_to_all(
        jnp.broadcast_to(own_half[None], (seq_count,) + own_half.shape),
        "seq",
        split_axis=0,
        concat_axis=0,
        tiled=True,
    ).reshape((-1,) + own_half.shape[1:])
    qkv = jnp.einsum("td,dshe->tshe", group_normed, w_qkv, preferred_element_type=jnp.float32)
    query = rotary(qkv[:, 0], offset).astype(jnp.bfloat16)
    keys = rotary(qkv[:, 1], offset).astype(jnp.bfloat16)
    values = qkv[:, 2].astype(jnp.bfloat16)
    block_count = 4
    block_rows = group_tokens // block_count
    key_places = jnp.arange(group_tokens, dtype=jnp.int32)

    def one_block(block_index):
        first_row = block_index * block_rows
        key_count = first_row + block_rows
        block_query = query[first_row:key_count]
        block_segment = segment[first_row:key_count]
        query_places = key_places[first_row:key_count]
        scores = (
            jnp.einsum(
                "qhd,khd->hqk", block_query, keys[:key_count], preferred_element_type=jnp.float32
            )
            * scale_factor
        )
        allowed = (block_segment[:, None] == segment[None, :key_count]) & (
            key_places[None, :key_count] <= query_places[:, None]
        )
        scores = jnp.where(allowed[None], scores, -1e30)
        highest = jnp.max(scores, axis=2, keepdims=True)
        weights = jnp.exp(scores - highest)
        probs = (weights / jnp.sum(weights, axis=2, keepdims=True)).astype(jnp.bfloat16)
        return jnp.einsum(
            "hqk,khd->qhd", probs, values[:key_count], preferred_element_type=jnp.float32
        ).astype(jnp.bfloat16)

    blocks = jnp.concatenate([one_block(index) for index in range(block_count)], axis=0)
    own_weight, blocks = lax.optimization_barrier((own_weight, blocks))
    heads_flat = blocks.reshape(group_tokens, head_count * head_size)
    regrouped = lax.all_to_all(heads_flat, "seq", split_axis=0, concat_axis=1, tiled=True)
    other_weight = pair_swap(own_weight)
    regrouped = regrouped.reshape(tok_rows, -1, head_size)
    own_heads = lax.dynamic_slice_in_dim(regrouped, core * half_size, half_size, axis=2)
    other_heads = lax.dynamic_slice_in_dim(regrouped, (1 - core) * half_size, half_size, axis=2)
    mixed = jnp.einsum(
        "thd,hdo->to", own_heads, own_weight, preferred_element_type=jnp.float32
    ) + jnp.einsum("thd,hdo->to", other_heads, other_weight, preferred_element_type=jnp.float32)
    middle = (token_rows.astype(jnp.float32) + mixed).astype(jnp.bfloat16)
    expert_in = rms_scale(middle, moe_gain).astype(jnp.bfloat16)
    logits = jnp.dot(expert_in, router, preferred_element_type=jnp.float32)
    expert_count = router.shape[1]
    token_routes = routes[0]
    top_count = token_routes.shape[1]
    expert_ids = jnp.arange(expert_count, dtype=jnp.int32)
    chosen_mask = token_routes[:, :, None] == expert_ids[None, None, :]
    chosen = jnp.sum(jnp.where(chosen_mask, logits[:, None, :], 0.0), axis=2)
    gates = jax.nn.softmax(chosen, axis=-1)
    capacity = max(2, tok_rows * top_count * 7 // (6 * expert_count))
    flat_mask = chosen_mask.reshape(tok_rows * top_count, expert_count).astype(jnp.int32)
    earlier_count = jnp.cumsum(flat_mask, axis=0) - flat_mask
    slot_index = jnp.sum(earlier_count * flat_mask, axis=1)
    target = (token_routes.reshape(-1) * capacity + slot_index).reshape(tok_rows, top_count)
    slot_total = expert_count * capacity
    placed = target[:, :, None] == jnp.arange(slot_total, dtype=jnp.int32)[None, None, :]
    shares = device_count // expert_count
    assert capacity % shares == 0
    per_dest = capacity // shares
    dispatch_table = jnp.any(placed, axis=1).astype(jnp.bfloat16)
    dispatch_table = dispatch_table.reshape(tok_rows, device_count, per_dest)
    slot_weights = jnp.sum(jnp.where(placed, gates[:, :, None], 0.0), axis=1)
    slot_weights = slot_weights.reshape(tok_rows, device_count, per_dest)
    gate_up = w_gate_up[0]
    down_weight = w_down[0]
    other_gate_up = pair_swap(gate_up)
    other_down = pair_swap(down_weight)

    def share_part(rows, pair, down):
        both = jnp.einsum("scd,gfd->scgf", rows, pair, preferred_element_type=jnp.float32)
        act = (jax.nn.silu(both[:, :, 0]) * both[:, :, 1]).astype(jnp.bfloat16)
        part = jnp.einsum("scf,fd->scd", act, down, preferred_element_type=jnp.float32)
        return part.astype(jnp.bfloat16).astype(jnp.float32)

    cuts = [0, per_dest // 2, per_dest]
    routed = jnp.zeros((tok_rows, model_width), jnp.float32)
    for low, high in zip(cuts[:-1], cuts[1:]):
        outgoing = jnp.einsum(
            "tsc,tm->scm",
            dispatch_table[:, :, low:high],
            expert_in,
            preferred_element_type=jnp.float32,
        ).astype(jnp.bfloat16)
        arrived = lax.all_to_all(
            outgoing, ("seq", "exp"), split_axis=0, concat_axis=0, tiled=True
        )
        part_sum = share_part(arrived, gate_up, down_weight) + share_part(
            arrived, other_gate_up, other_down
        )
        returned = lax.all_to_all(
            part_sum.astype(jnp.bfloat16), ("seq", "exp"), split_axis=0, concat_axis=0, tiled=True
        )
        routed = routed + jnp.einsum(
            "tsc,scm->tm",
            slot_weights[:, :, low:high],
            returned.astype(jnp.float32),
            precision=lax.Precision.HIGHEST,
            preferred_element_type=jnp.float32,
        )
    layer_rows = (middle.astype(jnp.float32) + routed).astype(jnp.bfloat16)
    prompt_count = prompt_lengths.shape[0]
    last_places = jnp.cumsum(prompt_lengths) - 1
    here_places = lax.axis_index("seq") * tok_rows + jnp.arange(tok_rows, dtype=jnp.int32)
    select_table = (last_places[:, None] == here_places[None, :]).astype(jnp.bfloat16)
    picked = jnp.dot(select_table, layer_rows, preferred_element_type=jnp.float32)
    outgoing_rows = jnp.broadcast_to(
        picked.astype(jnp.bfloat16)[None], (device_count, prompt_count, model_width)
    )
    arrived_rows = lax.all_to_all(
        outgoing_rows, ("seq", "exp"), split_axis=0, concat_axis=0, tiled=True
    ).astype(jnp.float32)
    last_rows = jnp.sum(
        arrived_rows.reshape(seq_count, group_count * prompt_count, model_width), axis=0
    )
    final = rms_scale(last_rows, final_gain).astype(jnp.bfloat16)
    vocab_scores = lax.dot_general(
        final, lm_head, (((1,), (1,)), ((), ())), preferred_element_type=jnp.float32
    )
    local_peak = jnp.max(vocab_scores, axis=1)
    local_total = jnp.sum(jnp.exp(vocab_scores - local_peak[:, None]), axis=1)
    local_stats = jnp.stack([local_peak, local_total])
    all_stats = lax.all_to_all(
        jnp.broadcast_to(local_stats[None], (device_count,) + local_stats.shape),
        ("seq", "exp"),
        split_axis=0,
        concat_axis=0,
        tiled=True,
    )
    all_peaks = all_stats[:, 0]
    global_peak = jnp.max(all_peaks, axis=0)
    global_total = jnp.sum(all_stats[:, 1] * jnp.exp(all_peaks - global_peak[None]), axis=0)
    logprobs = vocab_scores - (global_peak + jnp.log(global_total))[:, None]
    return (layer_rows[None], logprobs)


def solution(mesh):
    return jax.shard_map(
        per_device,
        mesh=mesh,
        in_specs=(
            P("exp", "seq", None),
            P("exp", None),
            P(),
            P(None, None, "seq", None),
            P("seq", None, None),
            P(),
            P(),
            P("exp", "seq", None),
            P(("seq", "exp"), None, None, None),
            P(("seq", "exp"), None, None),
            P(),
            P(("seq", "exp"), None),
        ),
        out_specs=(P("exp", "seq", None), P(None, ("seq", "exp"))),
        check_vma=False,
    )
```

```python
import jax
import jax.numpy as jnp
from jax import lax
from jax.sharding import PartitionSpec as P

epsilon = 1e-06


def joined(value, axis, join):
    pieces = jax.tree.map(lambda part: lax.all_gather(part, axis), value)
    head = jax.tree.map(lambda part: part[0], pieces)
    tail = jax.tree.map(lambda part: part[1:], pieces)
    subtotal, _ = lax.scan(lambda subtotal, piece: (join(subtotal, piece), None), head, tail)
    return subtotal


def rms_scale(values, gain):
    widened = values.astype(jnp.float32)
    inverse = lax.rsqrt(jnp.mean(widened * widened, axis=-1, keepdims=True) + epsilon)
    return widened * inverse * gain


def segment_layout(prompt_lengths, count):
    ends = jnp.cumsum(prompt_lengths)
    starts = ends - prompt_lengths
    places = jnp.arange(count, dtype=jnp.int32)
    member = ((places[:, None] >= starts[None, :]) & (places[:, None] < ends[None, :])).astype(
        jnp.int32
    )
    numbers = jnp.arange(prompt_lengths.shape[0], dtype=jnp.int32)
    segment = jnp.sum(member * numbers[None, :], axis=1)
    offset = places - jnp.sum(member * starts[None, :], axis=1)
    return (segment, offset)


def rotary(values, positions):
    half_size = values.shape[-1] // 2
    freqs = 10000.0 ** (-2.0 * jnp.arange(half_size, dtype=jnp.float32) / values.shape[-1])
    angles = positions.astype(jnp.float32)[:, None] * freqs[None, :]
    cosine = jnp.cos(angles)[:, None, :]
    sine = jnp.sin(angles)[:, None, :]
    first_half = values[..., :half_size]
    second_half = values[..., half_size:]
    return jnp.concatenate(
        [first_half * cosine - second_half * sine, second_half * cosine + first_half * sine],
        axis=-1,
    )


def pair_swap(value):
    count = lax.axis_size("exp")
    return lax.ppermute(value, "exp", [(i, i ^ 1) for i in range(count)])


def merge_softmax(earlier, later):
    highest = jnp.maximum(earlier[0], later[0])
    return (
        highest,
        earlier[1] * jnp.exp(earlier[0] - highest) + later[1] * jnp.exp(later[0] - highest),
    )


def per_device(
    hidden,
    lengths,
    attn_gain,
    w_qkv,
    w_out,
    moe_gain,
    router,
    routes,
    w_gate_up,
    w_down,
    final_gain,
    lm_head,
):
    seq_count = lax.axis_size("seq")
    group_count = lax.axis_size("exp")
    device_count = seq_count * group_count
    token_rows = hidden[0]
    tok_rows = token_rows.shape[0]
    model_width = token_rows.shape[1]
    group_tokens = tok_rows * seq_count
    head_count = w_qkv.shape[2]
    head_size = w_qkv.shape[3]
    scale_factor = head_size ** (-0.5)
    prompt_lengths = lengths[0]
    segment, offset = segment_layout(prompt_lengths, group_tokens)
    normed = rms_scale(token_rows, attn_gain).astype(jnp.bfloat16)
    group_normed = lax.all_gather(normed, "seq", axis=0, tiled=True)
    part_size = head_size // group_count
    own_part = lax.dynamic_slice_in_dim(
        w_out, lax.axis_index("exp") * part_size, part_size, axis=1
    )
    seq_part = lax.all_to_all(
        jnp.broadcast_to(own_part[None], (seq_count,) + own_part.shape),
        "seq",
        split_axis=0,
        concat_axis=0,
        tiled=True,
    ).reshape((1, -1) + own_part.shape[1:])
    qkv = jnp.einsum("td,dshe->tshe", group_normed, w_qkv, preferred_element_type=jnp.float32)
    query = rotary(qkv[:, 0], offset).astype(jnp.bfloat16)
    keys = rotary(qkv[:, 1], offset).astype(jnp.bfloat16)
    values = qkv[:, 2].astype(jnp.bfloat16)
    block_count = 4
    block_rows = group_tokens // block_count
    key_places = jnp.arange(group_tokens, dtype=jnp.int32)

    def one_block(block_index):
        first_row = block_index * block_rows
        key_count = first_row + block_rows
        block_query = query[first_row:key_count]
        block_segment = segment[first_row:key_count]
        query_places = key_places[first_row:key_count]
        scores = (
            jnp.einsum(
                "qhd,khd->hqk", block_query, keys[:key_count], preferred_element_type=jnp.float32
            )
            * scale_factor
        )
        allowed = (block_segment[:, None] == segment[None, :key_count]) & (
            key_places[None, :key_count] <= query_places[:, None]
        )
        scores = jnp.where(allowed[None], scores, -1e30)
        highest = jnp.max(scores, axis=2, keepdims=True)
        weights = jnp.exp(scores - highest)
        probs = (weights / jnp.sum(weights, axis=2, keepdims=True)).astype(jnp.bfloat16)
        return jnp.einsum(
            "hqk,khd->qhd", probs, values[:key_count], preferred_element_type=jnp.float32
        ).astype(jnp.bfloat16)

    blocks = jnp.concatenate([one_block(index) for index in range(block_count)], axis=0)
    heads_flat = blocks.reshape(group_tokens, head_count * head_size)
    regrouped = lax.all_to_all(heads_flat, "seq", split_axis=0, concat_axis=1, tiled=True)
    exp_index = lax.axis_index("exp")
    x_count = group_count // 2
    pieces, owners = [seq_part[0]], [exp_index]
    for step in range(1, x_count):
        pieces.append(
            lax.ppermute(
                seq_part[0],
                "exp",
                [(i, (i + 2 * step) % group_count) for i in range(group_count)],
            )
        )
        owners.append((exp_index - 2 * step) % group_count)
    partner_pieces = pair_swap(jnp.stack(pieces))
    pieces = pieces + [partner_pieces[step] for step in range(x_count)]
    owners = owners + [owner ^ 1 for owner in owners]
    regrouped = regrouped.reshape(tok_rows, -1, group_count, part_size)
    mixed = jnp.zeros((tok_rows, model_width), jnp.float32)
    for piece, owner in zip(pieces, owners):
        mixed = mixed + jnp.einsum(
            "thd,hdo->to",
            lax.dynamic_index_in_dim(regrouped, owner, axis=2, keepdims=False),
            piece,
            preferred_element_type=jnp.float32,
        )
    middle = (token_rows.astype(jnp.float32) + mixed).astype(jnp.bfloat16)
    expert_in = rms_scale(middle, moe_gain).astype(jnp.bfloat16)
    logits = jnp.dot(expert_in, router, preferred_element_type=jnp.float32)
    expert_count = router.shape[1]
    token_routes = routes[0]
    top_count = token_routes.shape[1]
    expert_ids = jnp.arange(expert_count, dtype=jnp.int32)
    chosen_mask = token_routes[:, :, None] == expert_ids[None, None, :]
    chosen = jnp.sum(jnp.where(chosen_mask, logits[:, None, :], 0.0), axis=2)
    gates = jax.nn.softmax(chosen, axis=-1)
    capacity = max(2, tok_rows * top_count * 7 // (6 * expert_count))
    flat_mask = chosen_mask.reshape(tok_rows * top_count, expert_count).astype(jnp.int32)
    earlier_count = jnp.cumsum(flat_mask, axis=0) - flat_mask
    slot_index = jnp.sum(earlier_count * flat_mask, axis=1)
    target = (token_routes.reshape(-1) * capacity + slot_index).reshape(tok_rows, top_count)
    slot_total = expert_count * capacity
    placed = target[:, :, None] == jnp.arange(slot_total, dtype=jnp.int32)[None, None, :]
    shares = device_count // expert_count
    assert capacity % shares == 0
    per_dest = capacity // shares
    dispatch_table = jnp.any(placed, axis=1).astype(jnp.bfloat16)
    dispatch_table = dispatch_table.reshape(tok_rows, device_count, per_dest)
    slot_weights = jnp.sum(jnp.where(placed, gates[:, :, None], 0.0), axis=1)
    slot_weights = slot_weights.reshape(tok_rows, device_count, per_dest)
    gate_up = w_gate_up[0]
    down_weight = w_down[0]
    other_gate_up = pair_swap(gate_up)
    other_down = pair_swap(down_weight)

    def share_part(rows, pair, down):
        both = jnp.einsum("scd,gfd->scgf", rows, pair, preferred_element_type=jnp.float32)
        act = (jax.nn.silu(both[:, :, 0]) * both[:, :, 1]).astype(jnp.bfloat16)
        part = jnp.einsum("scf,fd->scd", act, down, preferred_element_type=jnp.float32)
        return part.astype(jnp.bfloat16).astype(jnp.float32)

    cuts = [0, per_dest // 2, per_dest]
    routed = jnp.zeros((tok_rows, model_width), jnp.float32)
    for low, high in zip(cuts[:-1], cuts[1:]):
        outgoing = jnp.einsum(
            "tsc,tm->scm",
            dispatch_table[:, :, low:high],
            expert_in,
            preferred_element_type=jnp.float32,
        ).astype(jnp.bfloat16)
        arrived = lax.all_to_all(
            outgoing, ("seq", "exp"), split_axis=0, concat_axis=0, tiled=True
        )
        part_sum = share_part(arrived, gate_up, down_weight) + share_part(
            arrived, other_gate_up, other_down
        )
        returned = lax.all_to_all(
            part_sum.astype(jnp.bfloat16), ("seq", "exp"), split_axis=0, concat_axis=0, tiled=True
        )
        routed = routed + jnp.einsum(
            "tsc,scm->tm",
            slot_weights[:, :, low:high],
            returned.astype(jnp.float32),
            precision=lax.Precision.HIGHEST,
            preferred_element_type=jnp.float32,
        )
    layer_rows = (middle.astype(jnp.float32) + routed).astype(jnp.bfloat16)
    prompt_count = prompt_lengths.shape[0]
    last_places = jnp.cumsum(prompt_lengths) - 1
    here_places = lax.axis_index("seq") * tok_rows + jnp.arange(tok_rows, dtype=jnp.int32)
    select_table = (last_places[:, None] == here_places[None, :]).astype(jnp.bfloat16)
    picked = jnp.dot(select_table, layer_rows, preferred_element_type=jnp.float32)
    outgoing_rows = jnp.broadcast_to(
        picked.astype(jnp.bfloat16)[None], (device_count, prompt_count, model_width)
    )
    arrived_rows = lax.all_to_all(
        outgoing_rows, ("seq", "exp"), split_axis=0, concat_axis=0, tiled=True
    ).astype(jnp.float32)
    last_rows = jnp.sum(
        arrived_rows.reshape(seq_count, group_count * prompt_count, model_width), axis=0
    )
    final = rms_scale(last_rows, final_gain).astype(jnp.bfloat16)
    vocab_scores = lax.dot_general(
        final, lm_head, (((1,), (1,)), ((), ())), preferred_element_type=jnp.float32
    )
    local_peak = jnp.max(vocab_scores, axis=1)
    local_total = jnp.sum(jnp.exp(vocab_scores - local_peak[:, None]), axis=1)
    local_stats = jnp.stack([local_peak, local_total])
    all_stats = lax.all_to_all(
        jnp.broadcast_to(local_stats[None], (device_count,) + local_stats.shape),
        ("seq", "exp"),
        split_axis=0,
        concat_axis=0,
        tiled=True,
    )
    all_peaks = all_stats[:, 0]
    global_peak = jnp.max(all_peaks, axis=0)
    global_total = jnp.sum(all_stats[:, 1] * jnp.exp(all_peaks - global_peak[None]), axis=0)
    logprobs = vocab_scores - (global_peak + jnp.log(global_total))[:, None]
    return (layer_rows[None], logprobs)


def solution(mesh):
    return jax.shard_map(
        per_device,
        mesh=mesh,
        in_specs=(
            P("exp", "seq", None),
            P("exp", None),
            P(),
            P(None, None, "seq", None),
            P("seq", None, None),
            P(),
            P(),
            P("exp", "seq", None),
            P(("seq", "exp"), None, None, None),
            P(("seq", "exp"), None, None),
            P(),
            P(("seq", "exp"), None),
        ),
        out_specs=(P("exp", "seq", None), P(None, ("seq", "exp"))),
        check_vma=False,
    )
```

```python
import jax
import jax.numpy as jnp
from jax import lax
from jax.sharding import PartitionSpec as P

epsilon = 1e-06


def joined(value, axis, join):
    pieces = jax.tree.map(lambda part: lax.all_gather(part, axis), value)
    head = jax.tree.map(lambda part: part[0], pieces)
    tail = jax.tree.map(lambda part: part[1:], pieces)
    subtotal, _ = lax.scan(lambda subtotal, piece: (join(subtotal, piece), None), head, tail)
    return subtotal


def rms_scale(values, gain):
    widened = values.astype(jnp.float32)
    inverse = lax.rsqrt(jnp.mean(widened * widened, axis=-1, keepdims=True) + epsilon)
    return widened * inverse * gain


def segment_layout(prompt_lengths, count):
    ends = jnp.cumsum(prompt_lengths)
    starts = ends - prompt_lengths
    places = jnp.arange(count, dtype=jnp.int32)
    member = ((places[:, None] >= starts[None, :]) & (places[:, None] < ends[None, :])).astype(
        jnp.int32
    )
    numbers = jnp.arange(prompt_lengths.shape[0], dtype=jnp.int32)
    segment = jnp.sum(member * numbers[None, :], axis=1)
    offset = places - jnp.sum(member * starts[None, :], axis=1)
    return (segment, offset)


def rotary(values, positions):
    half_size = values.shape[-1] // 2
    freqs = 10000.0 ** (-2.0 * jnp.arange(half_size, dtype=jnp.float32) / values.shape[-1])
    angles = positions.astype(jnp.float32)[:, None] * freqs[None, :]
    cosine = jnp.cos(angles)[:, None, :]
    sine = jnp.sin(angles)[:, None, :]
    first_half = values[..., :half_size]
    second_half = values[..., half_size:]
    return jnp.concatenate(
        [first_half * cosine - second_half * sine, second_half * cosine + first_half * sine],
        axis=-1,
    )


def pair_swap(value):
    count = lax.axis_size("exp")
    return lax.ppermute(value, "exp", [(i, i ^ 1) for i in range(count)])


def merge_softmax(earlier, later):
    highest = jnp.maximum(earlier[0], later[0])
    return (
        highest,
        earlier[1] * jnp.exp(earlier[0] - highest) + later[1] * jnp.exp(later[0] - highest),
    )


def per_device(
    hidden,
    lengths,
    attn_gain,
    w_qkv,
    w_out,
    moe_gain,
    router,
    routes,
    w_gate_up,
    w_down,
    final_gain,
    lm_head,
):
    seq_count = lax.axis_size("seq")
    group_count = lax.axis_size("exp")
    device_count = seq_count * group_count
    token_rows = hidden[0]
    tok_rows = token_rows.shape[0]
    model_width = token_rows.shape[1]
    group_tokens = tok_rows * seq_count
    head_count = w_qkv.shape[2]
    head_size = w_qkv.shape[3]
    scale_factor = head_size ** (-0.5)
    prompt_lengths = lengths[0]
    segment, offset = segment_layout(prompt_lengths, group_tokens)
    normed = rms_scale(token_rows, attn_gain).astype(jnp.bfloat16)
    group_normed = lax.all_gather(normed, "seq", axis=0, tiled=True)
    part_size = head_size // group_count
    own_part = lax.dynamic_slice_in_dim(
        w_out, lax.axis_index("exp") * part_size, part_size, axis=1
    )
    seq_part = lax.all_to_all(
        jnp.broadcast_to(own_part[None], (seq_count,) + own_part.shape),
        "seq",
        split_axis=0,
        concat_axis=0,
        tiled=True,
    ).reshape((1, -1) + own_part.shape[1:])
    exp_index = lax.axis_index("exp")
    x_count = group_count // 2
    x_pieces, x_owners = [], []
    for step in range(1, x_count):
        x_pieces.append(
            lax.ppermute(
                seq_part[0],
                "exp",
                [(i, (i + 2 * step) % group_count) for i in range(group_count)],
            )
        )
        x_owners.append((exp_index - 2 * step) % group_count)
    qkv = jnp.einsum("td,dshe->tshe", group_normed, w_qkv, preferred_element_type=jnp.float32)
    query = rotary(qkv[:, 0], offset).astype(jnp.bfloat16)
    keys = rotary(qkv[:, 1], offset).astype(jnp.bfloat16)
    values = qkv[:, 2].astype(jnp.bfloat16)
    block_count = 4
    block_rows = group_tokens // block_count
    key_places = jnp.arange(group_tokens, dtype=jnp.int32)

    def one_block(block_index):
        first_row = block_index * block_rows
        key_count = first_row + block_rows
        block_query = query[first_row:key_count]
        block_segment = segment[first_row:key_count]
        query_places = key_places[first_row:key_count]
        scores = (
            jnp.einsum(
                "qhd,khd->hqk", block_query, keys[:key_count], preferred_element_type=jnp.float32
            )
            * scale_factor
        )
        allowed = (block_segment[:, None] == segment[None, :key_count]) & (
            key_places[None, :key_count] <= query_places[:, None]
        )
        scores = jnp.where(allowed[None], scores, -1e30)
        highest = jnp.max(scores, axis=2, keepdims=True)
        weights = jnp.exp(scores - highest)
        probs = (weights / jnp.sum(weights, axis=2, keepdims=True)).astype(jnp.bfloat16)
        return jnp.einsum(
            "hqk,khd->qhd", probs, values[:key_count], preferred_element_type=jnp.float32
        ).astype(jnp.bfloat16)

    blocks = jnp.concatenate([one_block(index) for index in range(block_count)], axis=0)
    x_pieces, blocks = lax.optimization_barrier((x_pieces, blocks))
    heads_flat = blocks.reshape(group_tokens, head_count * head_size)
    regrouped = lax.all_to_all(heads_flat, "seq", split_axis=0, concat_axis=1, tiled=True)
    pieces, owners = [seq_part[0]] + x_pieces, [exp_index] + x_owners
    partner_pieces = pair_swap(jnp.stack(pieces))
    pieces = pieces + [partner_pieces[step] for step in range(x_count)]
    owners = owners + [owner ^ 1 for owner in owners]
    regrouped = regrouped.reshape(tok_rows, -1, group_count, part_size)
    mixed = jnp.zeros((tok_rows, model_width), jnp.float32)
    for piece, owner in zip(pieces, owners):
        mixed = mixed + jnp.einsum(
            "thd,hdo->to",
            lax.dynamic_index_in_dim(regrouped, owner, axis=2, keepdims=False),
            piece,
            preferred_element_type=jnp.float32,
        )
    middle = (token_rows.astype(jnp.float32) + mixed).astype(jnp.bfloat16)
    expert_in = rms_scale(middle, moe_gain).astype(jnp.bfloat16)
    logits = jnp.dot(expert_in, router, preferred_element_type=jnp.float32)
    expert_count = router.shape[1]
    token_routes = routes[0]
    top_count = token_routes.shape[1]
    expert_ids = jnp.arange(expert_count, dtype=jnp.int32)
    chosen_mask = token_routes[:, :, None] == expert_ids[None, None, :]
    chosen = jnp.sum(jnp.where(chosen_mask, logits[:, None, :], 0.0), axis=2)
    gates = jax.nn.softmax(chosen, axis=-1)
    capacity = max(2, tok_rows * top_count * 7 // (6 * expert_count))
    flat_mask = chosen_mask.reshape(tok_rows * top_count, expert_count).astype(jnp.int32)
    earlier_count = jnp.cumsum(flat_mask, axis=0) - flat_mask
    slot_index = jnp.sum(earlier_count * flat_mask, axis=1)
    target = (token_routes.reshape(-1) * capacity + slot_index).reshape(tok_rows, top_count)
    slot_total = expert_count * capacity
    placed = target[:, :, None] == jnp.arange(slot_total, dtype=jnp.int32)[None, None, :]
    shares = device_count // expert_count
    assert capacity % shares == 0
    per_dest = capacity // shares
    dispatch_table = jnp.any(placed, axis=1).astype(jnp.bfloat16)
    dispatch_table = dispatch_table.reshape(tok_rows, device_count, per_dest)
    slot_weights = jnp.sum(jnp.where(placed, gates[:, :, None], 0.0), axis=1)
    slot_weights = slot_weights.reshape(tok_rows, device_count, per_dest)
    gate_up = w_gate_up[0]
    down_weight = w_down[0]
    other_gate_up = pair_swap(gate_up)
    other_down = pair_swap(down_weight)

    def share_part(rows, pair, down):
        both = jnp.einsum("scd,gfd->scgf", rows, pair, preferred_element_type=jnp.float32)
        act = (jax.nn.silu(both[:, :, 0]) * both[:, :, 1]).astype(jnp.bfloat16)
        part = jnp.einsum("scf,fd->scd", act, down, preferred_element_type=jnp.float32)
        return part.astype(jnp.bfloat16).astype(jnp.float32)

    cuts = [0, per_dest // 2, per_dest]
    routed = jnp.zeros((tok_rows, model_width), jnp.float32)
    for low, high in zip(cuts[:-1], cuts[1:]):
        outgoing = jnp.einsum(
            "tsc,tm->scm",
            dispatch_table[:, :, low:high],
            expert_in,
            preferred_element_type=jnp.float32,
        ).astype(jnp.bfloat16)
        arrived = lax.all_to_all(
            outgoing, ("seq", "exp"), split_axis=0, concat_axis=0, tiled=True
        )
        part_sum = share_part(arrived, gate_up, down_weight) + share_part(
            arrived, other_gate_up, other_down
        )
        returned = lax.all_to_all(
            part_sum.astype(jnp.bfloat16), ("seq", "exp"), split_axis=0, concat_axis=0, tiled=True
        )
        routed = routed + jnp.einsum(
            "tsc,scm->tm",
            slot_weights[:, :, low:high],
            returned.astype(jnp.float32),
            precision=lax.Precision.HIGHEST,
            preferred_element_type=jnp.float32,
        )
    layer_rows = (middle.astype(jnp.float32) + routed).astype(jnp.bfloat16)
    prompt_count = prompt_lengths.shape[0]
    last_places = jnp.cumsum(prompt_lengths) - 1
    here_places = lax.axis_index("seq") * tok_rows + jnp.arange(tok_rows, dtype=jnp.int32)
    select_table = (last_places[:, None] == here_places[None, :]).astype(jnp.bfloat16)
    picked = jnp.dot(select_table, layer_rows, preferred_element_type=jnp.float32)
    outgoing_rows = jnp.broadcast_to(
        picked.astype(jnp.bfloat16)[None], (device_count, prompt_count, model_width)
    )
    arrived_rows = lax.all_to_all(
        outgoing_rows, ("seq", "exp"), split_axis=0, concat_axis=0, tiled=True
    ).astype(jnp.float32)
    last_rows = jnp.sum(
        arrived_rows.reshape(seq_count, group_count * prompt_count, model_width), axis=0
    )
    final = rms_scale(last_rows, final_gain).astype(jnp.bfloat16)
    vocab_scores = lax.dot_general(
        final, lm_head, (((1,), (1,)), ((), ())), preferred_element_type=jnp.float32
    )
    local_peak = jnp.max(vocab_scores, axis=1)
    local_total = jnp.sum(jnp.exp(vocab_scores - local_peak[:, None]), axis=1)
    local_stats = jnp.stack([local_peak, local_total])
    all_stats = lax.all_to_all(
        jnp.broadcast_to(local_stats[None], (device_count,) + local_stats.shape),
        ("seq", "exp"),
        split_axis=0,
        concat_axis=0,
        tiled=True,
    )
    all_peaks = all_stats[:, 0]
    global_peak = jnp.max(all_peaks, axis=0)
    global_total = jnp.sum(all_stats[:, 1] * jnp.exp(all_peaks - global_peak[None]), axis=0)
    logprobs = vocab_scores - (global_peak + jnp.log(global_total))[:, None]
    return (layer_rows[None], logprobs)


def solution(mesh):
    return jax.shard_map(
        per_device,
        mesh=mesh,
        in_specs=(
            P("exp", "seq", None),
            P("exp", None),
            P(),
            P(None, None, "seq", None),
            P("seq", None, None),
            P(),
            P(),
            P("exp", "seq", None),
            P(("seq", "exp"), None, None, None),
            P(("seq", "exp"), None, None),
            P(),
            P(("seq", "exp"), None),
        ),
        out_specs=(P("exp", "seq", None), P(None, ("seq", "exp"))),
        check_vma=False,
    )
```

```python
import jax
import jax.numpy as jnp
from jax import lax
from jax.sharding import PartitionSpec as P

epsilon = 1e-06


def joined(value, axis, join):
    pieces = jax.tree.map(lambda part: lax.all_gather(part, axis), value)
    head = jax.tree.map(lambda part: part[0], pieces)
    tail = jax.tree.map(lambda part: part[1:], pieces)
    subtotal, _ = lax.scan(lambda subtotal, piece: (join(subtotal, piece), None), head, tail)
    return subtotal


def rms_scale(values, gain):
    widened = values.astype(jnp.float32)
    inverse = lax.rsqrt(jnp.mean(widened * widened, axis=-1, keepdims=True) + epsilon)
    return widened * inverse * gain


def segment_layout(prompt_lengths, count):
    ends = jnp.cumsum(prompt_lengths)
    starts = ends - prompt_lengths
    places = jnp.arange(count, dtype=jnp.int32)
    member = ((places[:, None] >= starts[None, :]) & (places[:, None] < ends[None, :])).astype(
        jnp.int32
    )
    numbers = jnp.arange(prompt_lengths.shape[0], dtype=jnp.int32)
    segment = jnp.sum(member * numbers[None, :], axis=1)
    offset = places - jnp.sum(member * starts[None, :], axis=1)
    return (segment, offset)


def rotary(values, positions):
    half_size = values.shape[-1] // 2
    freqs = 10000.0 ** (-2.0 * jnp.arange(half_size, dtype=jnp.float32) / values.shape[-1])
    angles = positions.astype(jnp.float32)[:, None] * freqs[None, :]
    cosine = jnp.cos(angles)[:, None, :]
    sine = jnp.sin(angles)[:, None, :]
    first_half = values[..., :half_size]
    second_half = values[..., half_size:]
    return jnp.concatenate(
        [first_half * cosine - second_half * sine, second_half * cosine + first_half * sine],
        axis=-1,
    )


def pair_swap(value):
    count = lax.axis_size("exp")
    return lax.ppermute(value, "exp", [(i, i ^ 1) for i in range(count)])


def merge_softmax(earlier, later):
    highest = jnp.maximum(earlier[0], later[0])
    return (
        highest,
        earlier[1] * jnp.exp(earlier[0] - highest) + later[1] * jnp.exp(later[0] - highest),
    )


def per_device(
    hidden,
    lengths,
    attn_gain,
    w_qkv,
    w_out,
    moe_gain,
    router,
    routes,
    w_gate_up,
    w_down,
    final_gain,
    lm_head,
):
    seq_count = lax.axis_size("seq")
    group_count = lax.axis_size("exp")
    device_count = seq_count * group_count
    token_rows = hidden[0]
    tok_rows = token_rows.shape[0]
    model_width = token_rows.shape[1]
    group_tokens = tok_rows * seq_count
    head_count = w_qkv.shape[2]
    head_size = w_qkv.shape[3]
    scale_factor = head_size ** (-0.5)
    prompt_lengths = lengths[0]
    segment, offset = segment_layout(prompt_lengths, group_tokens)
    normed = rms_scale(token_rows, attn_gain).astype(jnp.bfloat16)
    group_normed = lax.all_gather(normed, "seq", axis=0, tiled=True)
    part_size = head_size // group_count
    own_part = lax.dynamic_slice_in_dim(
        w_out, lax.axis_index("exp") * part_size, part_size, axis=1
    )
    own_part, group_normed = lax.optimization_barrier((own_part, group_normed))
    seq_part = lax.all_to_all(
        jnp.broadcast_to(own_part[None], (seq_count,) + own_part.shape),
        "seq",
        split_axis=0,
        concat_axis=0,
        tiled=True,
    ).reshape((1, -1) + own_part.shape[1:])
    exp_index = lax.axis_index("exp")
    x_count = group_count // 2
    x_pieces, x_owners = [], []
    for step in range(1, x_count):
        x_pieces.append(
            lax.ppermute(
                seq_part[0],
                "exp",
                [(i, (i + 2 * step) % group_count) for i in range(group_count)],
            )
        )
        x_owners.append((exp_index - 2 * step) % group_count)
    qkv = jnp.einsum("td,dshe->tshe", group_normed, w_qkv, preferred_element_type=jnp.float32)
    query = rotary(qkv[:, 0], offset).astype(jnp.bfloat16)
    keys = rotary(qkv[:, 1], offset).astype(jnp.bfloat16)
    values = qkv[:, 2].astype(jnp.bfloat16)
    block_count = 4
    block_rows = group_tokens // block_count
    key_places = jnp.arange(group_tokens, dtype=jnp.int32)

    def one_block(block_index):
        first_row = block_index * block_rows
        key_count = first_row + block_rows
        block_query = query[first_row:key_count]
        block_segment = segment[first_row:key_count]
        query_places = key_places[first_row:key_count]
        scores = (
            jnp.einsum(
                "qhd,khd->hqk", block_query, keys[:key_count], preferred_element_type=jnp.float32
            )
            * scale_factor
        )
        allowed = (block_segment[:, None] == segment[None, :key_count]) & (
            key_places[None, :key_count] <= query_places[:, None]
        )
        scores = jnp.where(allowed[None], scores, -1e30)
        highest = jnp.max(scores, axis=2, keepdims=True)
        weights = jnp.exp(scores - highest)
        probs = (weights / jnp.sum(weights, axis=2, keepdims=True)).astype(jnp.bfloat16)
        return jnp.einsum(
            "hqk,khd->qhd", probs, values[:key_count], preferred_element_type=jnp.float32
        ).astype(jnp.bfloat16)

    blocks = jnp.concatenate([one_block(index) for index in range(block_count)], axis=0)
    heads_flat = blocks.reshape(group_tokens, head_count * head_size)
    regrouped = lax.all_to_all(heads_flat, "seq", split_axis=0, concat_axis=1, tiled=True)
    x_pieces, regrouped = lax.optimization_barrier((x_pieces, regrouped))
    pieces, owners = [seq_part[0]] + x_pieces, [exp_index] + x_owners
    partner_pieces = pair_swap(jnp.stack(pieces))
    pieces = pieces + [partner_pieces[step] for step in range(x_count)]
    owners = owners + [owner ^ 1 for owner in owners]
    regrouped = regrouped.reshape(tok_rows, -1, group_count, part_size)
    mixed = jnp.zeros((tok_rows, model_width), jnp.float32)
    for piece, owner in zip(pieces, owners):
        mixed = mixed + jnp.einsum(
            "thd,hdo->to",
            lax.dynamic_index_in_dim(regrouped, owner, axis=2, keepdims=False),
            piece,
            preferred_element_type=jnp.float32,
        )
    middle = (token_rows.astype(jnp.float32) + mixed).astype(jnp.bfloat16)
    expert_in = rms_scale(middle, moe_gain).astype(jnp.bfloat16)
    logits = jnp.dot(expert_in, router, preferred_element_type=jnp.float32)
    expert_count = router.shape[1]
    token_routes = routes[0]
    top_count = token_routes.shape[1]
    expert_ids = jnp.arange(expert_count, dtype=jnp.int32)
    chosen_mask = token_routes[:, :, None] == expert_ids[None, None, :]
    chosen = jnp.sum(jnp.where(chosen_mask, logits[:, None, :], 0.0), axis=2)
    gates = jax.nn.softmax(chosen, axis=-1)
    capacity = max(2, tok_rows * top_count * 7 // (6 * expert_count))
    flat_mask = chosen_mask.reshape(tok_rows * top_count, expert_count).astype(jnp.int32)
    earlier_count = jnp.cumsum(flat_mask, axis=0) - flat_mask
    slot_index = jnp.sum(earlier_count * flat_mask, axis=1)
    target = (token_routes.reshape(-1) * capacity + slot_index).reshape(tok_rows, top_count)
    slot_total = expert_count * capacity
    placed = target[:, :, None] == jnp.arange(slot_total, dtype=jnp.int32)[None, None, :]
    shares = device_count // expert_count
    assert capacity % shares == 0
    per_dest = capacity // shares
    dispatch_table = jnp.any(placed, axis=1).astype(jnp.bfloat16)
    dispatch_table = dispatch_table.reshape(tok_rows, device_count, per_dest)
    slot_weights = jnp.sum(jnp.where(placed, gates[:, :, None], 0.0), axis=1)
    slot_weights = slot_weights.reshape(tok_rows, device_count, per_dest)
    gate_up = w_gate_up[0]
    down_weight = w_down[0]
    other_gate_up = pair_swap(gate_up)
    other_down = pair_swap(down_weight)

    def share_part(rows, pair, down):
        both = jnp.einsum("scd,gfd->scgf", rows, pair, preferred_element_type=jnp.float32)
        act = (jax.nn.silu(both[:, :, 0]) * both[:, :, 1]).astype(jnp.bfloat16)
        part = jnp.einsum("scf,fd->scd", act, down, preferred_element_type=jnp.float32)
        return part.astype(jnp.bfloat16).astype(jnp.float32)

    cuts = [0, per_dest // 2, per_dest]
    routed = jnp.zeros((tok_rows, model_width), jnp.float32)
    for low, high in zip(cuts[:-1], cuts[1:]):
        outgoing = jnp.einsum(
            "tsc,tm->scm",
            dispatch_table[:, :, low:high],
            expert_in,
            preferred_element_type=jnp.float32,
        ).astype(jnp.bfloat16)
        arrived = lax.all_to_all(
            outgoing, ("seq", "exp"), split_axis=0, concat_axis=0, tiled=True
        )
        part_sum = share_part(arrived, gate_up, down_weight) + share_part(
            arrived, other_gate_up, other_down
        )
        returned = lax.all_to_all(
            part_sum.astype(jnp.bfloat16), ("seq", "exp"), split_axis=0, concat_axis=0, tiled=True
        )
        routed = routed + jnp.einsum(
            "tsc,scm->tm",
            slot_weights[:, :, low:high],
            returned.astype(jnp.float32),
            precision=lax.Precision.HIGHEST,
            preferred_element_type=jnp.float32,
        )
    layer_rows = (middle.astype(jnp.float32) + routed).astype(jnp.bfloat16)
    prompt_count = prompt_lengths.shape[0]
    last_places = jnp.cumsum(prompt_lengths) - 1
    here_places = lax.axis_index("seq") * tok_rows + jnp.arange(tok_rows, dtype=jnp.int32)
    select_table = (last_places[:, None] == here_places[None, :]).astype(jnp.bfloat16)
    picked = jnp.dot(select_table, layer_rows, preferred_element_type=jnp.float32)
    outgoing_rows = jnp.broadcast_to(
        picked.astype(jnp.bfloat16)[None], (device_count, prompt_count, model_width)
    )
    arrived_rows = lax.all_to_all(
        outgoing_rows, ("seq", "exp"), split_axis=0, concat_axis=0, tiled=True
    ).astype(jnp.float32)
    last_rows = jnp.sum(
        arrived_rows.reshape(seq_count, group_count * prompt_count, model_width), axis=0
    )
    final = rms_scale(last_rows, final_gain).astype(jnp.bfloat16)
    vocab_scores = lax.dot_general(
        final, lm_head, (((1,), (1,)), ((), ())), preferred_element_type=jnp.float32
    )
    local_peak = jnp.max(vocab_scores, axis=1)
    local_total = jnp.sum(jnp.exp(vocab_scores - local_peak[:, None]), axis=1)
    local_stats = jnp.stack([local_peak, local_total])
    all_stats = lax.all_to_all(
        jnp.broadcast_to(local_stats[None], (device_count,) + local_stats.shape),
        ("seq", "exp"),
        split_axis=0,
        concat_axis=0,
        tiled=True,
    )
    all_peaks = all_stats[:, 0]
    global_peak = jnp.max(all_peaks, axis=0)
    global_total = jnp.sum(all_stats[:, 1] * jnp.exp(all_peaks - global_peak[None]), axis=0)
    logprobs = vocab_scores - (global_peak + jnp.log(global_total))[:, None]
    return (layer_rows[None], logprobs)


def solution(mesh):
    return jax.shard_map(
        per_device,
        mesh=mesh,
        in_specs=(
            P("exp", "seq", None),
            P("exp", None),
            P(),
            P(None, None, "seq", None),
            P("seq", None, None),
            P(),
            P(),
            P("exp", "seq", None),
            P(("seq", "exp"), None, None, None),
            P(("seq", "exp"), None, None),
            P(),
            P(("seq", "exp"), None),
        ),
        out_specs=(P("exp", "seq", None), P(None, ("seq", "exp"))),
        check_vma=False,
    )
```

```python
import jax
import jax.numpy as jnp
from jax import lax
from jax.sharding import PartitionSpec as P

epsilon = 1e-06


def joined(value, axis, join):
    pieces = jax.tree.map(lambda part: lax.all_gather(part, axis), value)
    head = jax.tree.map(lambda part: part[0], pieces)
    tail = jax.tree.map(lambda part: part[1:], pieces)
    subtotal, _ = lax.scan(lambda subtotal, piece: (join(subtotal, piece), None), head, tail)
    return subtotal


def rms_scale(values, gain):
    widened = values.astype(jnp.float32)
    inverse = lax.rsqrt(jnp.mean(widened * widened, axis=-1, keepdims=True) + epsilon)
    return widened * inverse * gain


def segment_layout(prompt_lengths, count):
    ends = jnp.cumsum(prompt_lengths)
    starts = ends - prompt_lengths
    places = jnp.arange(count, dtype=jnp.int32)
    member = ((places[:, None] >= starts[None, :]) & (places[:, None] < ends[None, :])).astype(
        jnp.int32
    )
    numbers = jnp.arange(prompt_lengths.shape[0], dtype=jnp.int32)
    segment = jnp.sum(member * numbers[None, :], axis=1)
    offset = places - jnp.sum(member * starts[None, :], axis=1)
    return (segment, offset)


def rotary(values, positions):
    half_size = values.shape[-1] // 2
    freqs = 10000.0 ** (-2.0 * jnp.arange(half_size, dtype=jnp.float32) / values.shape[-1])
    angles = positions.astype(jnp.float32)[:, None] * freqs[None, :]
    cosine = jnp.cos(angles)[:, None, :]
    sine = jnp.sin(angles)[:, None, :]
    first_half = values[..., :half_size]
    second_half = values[..., half_size:]
    return jnp.concatenate(
        [first_half * cosine - second_half * sine, second_half * cosine + first_half * sine],
        axis=-1,
    )


def pair_swap(value):
    count = lax.axis_size("exp")
    return lax.ppermute(value, "exp", [(i, i ^ 1) for i in range(count)])


def merge_softmax(earlier, later):
    highest = jnp.maximum(earlier[0], later[0])
    return (
        highest,
        earlier[1] * jnp.exp(earlier[0] - highest) + later[1] * jnp.exp(later[0] - highest),
    )


def per_device(
    hidden,
    lengths,
    attn_gain,
    w_qkv,
    w_out,
    moe_gain,
    router,
    routes,
    w_gate_up,
    w_down,
    final_gain,
    lm_head,
):
    seq_count = lax.axis_size("seq")
    group_count = lax.axis_size("exp")
    device_count = seq_count * group_count
    token_rows = hidden[0]
    tok_rows = token_rows.shape[0]
    model_width = token_rows.shape[1]
    group_tokens = tok_rows * seq_count
    head_count = w_qkv.shape[2]
    head_size = w_qkv.shape[3]
    scale_factor = head_size ** (-0.5)
    prompt_lengths = lengths[0]
    segment, offset = segment_layout(prompt_lengths, group_tokens)
    normed = rms_scale(token_rows, attn_gain).astype(jnp.bfloat16)
    group_normed = lax.all_gather(normed, "seq", axis=0, tiled=True)
    part_size = head_size // group_count
    own_part = lax.dynamic_slice_in_dim(
        w_out, lax.axis_index("exp") * part_size, part_size, axis=1
    )
    seq_part = lax.all_to_all(
        jnp.broadcast_to(own_part[None], (seq_count,) + own_part.shape),
        "seq",
        split_axis=0,
        concat_axis=0,
        tiled=True,
    ).reshape((1, -1) + own_part.shape[1:])
    exp_index = lax.axis_index("exp")
    x_count = group_count // 2
    x_pieces, x_owners = [], []
    for step in range(1, x_count):
        x_pieces.append(
            lax.ppermute(
                seq_part[0],
                "exp",
                [(i, (i + 2 * step) % group_count) for i in range(group_count)],
            )
        )
        x_owners.append((exp_index - 2 * step) % group_count)
    qkv = jnp.einsum("td,dshe->tshe", group_normed, w_qkv, preferred_element_type=jnp.float32)
    query = rotary(qkv[:, 0], offset).astype(jnp.bfloat16)
    keys = rotary(qkv[:, 1], offset).astype(jnp.bfloat16)
    values = qkv[:, 2].astype(jnp.bfloat16)
    block_count = 4
    block_rows = group_tokens // block_count
    key_places = jnp.arange(group_tokens, dtype=jnp.int32)

    def one_block(block_index):
        first_row = block_index * block_rows
        key_count = first_row + block_rows
        block_query = query[first_row:key_count]
        block_segment = segment[first_row:key_count]
        query_places = key_places[first_row:key_count]
        scores = (
            jnp.einsum(
                "qhd,khd->hqk", block_query, keys[:key_count], preferred_element_type=jnp.float32
            )
            * scale_factor
        )
        allowed = (block_segment[:, None] == segment[None, :key_count]) & (
            key_places[None, :key_count] <= query_places[:, None]
        )
        scores = jnp.where(allowed[None], scores, -1e30)
        highest = jnp.max(scores, axis=2, keepdims=True)
        weights = jnp.exp(scores - highest)
        probs = (weights / jnp.sum(weights, axis=2, keepdims=True)).astype(jnp.bfloat16)
        return jnp.einsum(
            "hqk,khd->qhd", probs, values[:key_count], preferred_element_type=jnp.float32
        ).astype(jnp.bfloat16)

    blocks = jnp.concatenate([one_block(index) for index in range(block_count)], axis=0)
    x_pieces, blocks = lax.optimization_barrier((x_pieces, blocks))
    heads_flat = blocks.reshape(group_tokens, head_count * head_size)
    regrouped = lax.all_to_all(heads_flat, "seq", split_axis=0, concat_axis=1, tiled=True)
    pieces, owners = [seq_part[0]] + x_pieces, [exp_index] + x_owners
    partner_pieces = pair_swap(jnp.stack(pieces))
    pieces = pieces + [partner_pieces[step] for step in range(x_count)]
    owners = owners + [owner ^ 1 for owner in owners]
    regrouped = regrouped.reshape(tok_rows, -1, group_count, part_size)
    mixed = jnp.zeros((tok_rows, model_width), jnp.float32)
    for piece, owner in zip(pieces, owners):
        mixed = mixed + jnp.einsum(
            "thd,hdo->to",
            lax.dynamic_index_in_dim(regrouped, owner, axis=2, keepdims=False),
            piece,
            preferred_element_type=jnp.float32,
        )
    middle = (token_rows.astype(jnp.float32) + mixed).astype(jnp.bfloat16)
    expert_in = rms_scale(middle, moe_gain).astype(jnp.bfloat16)
    logits = jnp.dot(expert_in, router, preferred_element_type=jnp.float32)
    expert_count = router.shape[1]
    token_routes = routes[0]
    top_count = token_routes.shape[1]
    expert_ids = jnp.arange(expert_count, dtype=jnp.int32)
    chosen_mask = token_routes[:, :, None] == expert_ids[None, None, :]
    chosen = jnp.sum(jnp.where(chosen_mask, logits[:, None, :], 0.0), axis=2)
    gates = jax.nn.softmax(chosen, axis=-1)
    capacity = max(2, tok_rows * top_count * 7 // (6 * expert_count))
    flat_mask = chosen_mask.reshape(tok_rows * top_count, expert_count).astype(jnp.int32)
    earlier_count = jnp.cumsum(flat_mask, axis=0) - flat_mask
    slot_index = jnp.sum(earlier_count * flat_mask, axis=1)
    target = (token_routes.reshape(-1) * capacity + slot_index).reshape(tok_rows, top_count)
    slot_total = expert_count * capacity
    placed = target[:, :, None] == jnp.arange(slot_total, dtype=jnp.int32)[None, None, :]
    shares = device_count // expert_count
    assert capacity % shares == 0
    per_dest = capacity // shares
    dispatch_table = jnp.any(placed, axis=1).astype(jnp.bfloat16)
    dispatch_table = dispatch_table.reshape(tok_rows, device_count, per_dest)
    slot_weights = jnp.sum(jnp.where(placed, gates[:, :, None], 0.0), axis=1)
    slot_weights = slot_weights.reshape(tok_rows, device_count, per_dest)
    gate_up = w_gate_up[0]
    down_weight = w_down[0]
    other_gate_up = pair_swap(gate_up)
    other_down = pair_swap(down_weight)

    def share_part(rows, pair, down):
        both = jnp.einsum("scd,gfd->scgf", rows, pair, preferred_element_type=jnp.float32)
        act = (jax.nn.silu(both[:, :, 0]) * both[:, :, 1]).astype(jnp.bfloat16)
        part = jnp.einsum("scf,fd->scd", act, down, preferred_element_type=jnp.float32)
        return part.astype(jnp.bfloat16).astype(jnp.float32)

    cuts = [0, per_dest // 2, per_dest]
    routed = jnp.zeros((tok_rows, model_width), jnp.float32)
    for low, high in zip(cuts[:-1], cuts[1:]):
        outgoing = jnp.einsum(
            "tsc,tm->scm",
            dispatch_table[:, :, low:high],
            expert_in,
            preferred_element_type=jnp.float32,
        ).astype(jnp.bfloat16)
        arrived = lax.all_to_all(
            outgoing, ("seq", "exp"), split_axis=0, concat_axis=0, tiled=True
        )
        part_sum = share_part(arrived, gate_up, down_weight) + share_part(
            arrived, other_gate_up, other_down
        )
        returned = lax.all_to_all(
            part_sum.astype(jnp.bfloat16), ("seq", "exp"), split_axis=0, concat_axis=0, tiled=True
        )
        routed = routed + jnp.einsum(
            "tsc,scm->tm",
            slot_weights[:, :, low:high],
            returned.astype(jnp.float32),
            precision=lax.Precision.HIGHEST,
            preferred_element_type=jnp.float32,
        )
    layer_rows = (middle.astype(jnp.float32) + routed).astype(jnp.bfloat16)
    prompt_count = prompt_lengths.shape[0]
    last_places = jnp.cumsum(prompt_lengths) - 1
    here_places = lax.axis_index("seq") * tok_rows + jnp.arange(tok_rows, dtype=jnp.int32)
    select_table = (last_places[:, None] == here_places[None, :]).astype(jnp.bfloat16)
    picked = jnp.dot(select_table, layer_rows, preferred_element_type=jnp.float32)
    group_rows = lax.all_to_all(
        jnp.broadcast_to(
            picked.astype(jnp.bfloat16)[None], (seq_count, prompt_count, model_width)
        ),
        "seq",
        split_axis=0,
        concat_axis=0,
        tiled=True,
    )
    group_rows = jnp.sum(group_rows.astype(jnp.float32), axis=0).astype(jnp.bfloat16)
    last_rows = lax.all_to_all(
        jnp.broadcast_to(group_rows[None], (group_count, prompt_count, model_width)),
        "exp",
        split_axis=0,
        concat_axis=0,
        tiled=True,
    ).reshape(group_count * prompt_count, model_width).astype(jnp.float32)
    final = rms_scale(last_rows, final_gain).astype(jnp.bfloat16)
    vocab_scores = lax.dot_general(
        final, lm_head, (((1,), (1,)), ((), ())), preferred_element_type=jnp.float32
    )
    local_peak = jnp.max(vocab_scores, axis=1)
    local_total = jnp.sum(jnp.exp(vocab_scores - local_peak[:, None]), axis=1)
    local_stats = jnp.stack([local_peak, local_total])
    all_stats = lax.all_to_all(
        jnp.broadcast_to(local_stats[None], (device_count,) + local_stats.shape),
        ("seq", "exp"),
        split_axis=0,
        concat_axis=0,
        tiled=True,
    )
    all_peaks = all_stats[:, 0]
    global_peak = jnp.max(all_peaks, axis=0)
    global_total = jnp.sum(all_stats[:, 1] * jnp.exp(all_peaks - global_peak[None]), axis=0)
    logprobs = vocab_scores - (global_peak + jnp.log(global_total))[:, None]
    return (layer_rows[None], logprobs)


def solution(mesh):
    return jax.shard_map(
        per_device,
        mesh=mesh,
        in_specs=(
            P("exp", "seq", None),
            P("exp", None),
            P(),
            P(None, None, "seq", None),
            P("seq", None, None),
            P(),
            P(),
            P("exp", "seq", None),
            P(("seq", "exp"), None, None, None),
            P(("seq", "exp"), None, None),
            P(),
            P(("seq", "exp"), None),
        ),
        out_specs=(P("exp", "seq", None), P(None, ("seq", "exp"))),
        check_vma=False,
    )
```

```python
import jax
import jax.numpy as jnp
from jax import lax
from jax.sharding import PartitionSpec as P

epsilon = 1e-06


def joined(value, axis, join):
    pieces = jax.tree.map(lambda part: lax.all_gather(part, axis), value)
    head = jax.tree.map(lambda part: part[0], pieces)
    tail = jax.tree.map(lambda part: part[1:], pieces)
    subtotal, _ = lax.scan(lambda subtotal, piece: (join(subtotal, piece), None), head, tail)
    return subtotal


def rms_scale(values, gain):
    widened = values.astype(jnp.float32)
    inverse = lax.rsqrt(jnp.mean(widened * widened, axis=-1, keepdims=True) + epsilon)
    return widened * inverse * gain


def segment_layout(prompt_lengths, count):
    ends = jnp.cumsum(prompt_lengths)
    starts = ends - prompt_lengths
    places = jnp.arange(count, dtype=jnp.int32)
    member = ((places[:, None] >= starts[None, :]) & (places[:, None] < ends[None, :])).astype(
        jnp.int32
    )
    numbers = jnp.arange(prompt_lengths.shape[0], dtype=jnp.int32)
    segment = jnp.sum(member * numbers[None, :], axis=1)
    offset = places - jnp.sum(member * starts[None, :], axis=1)
    return (segment, offset)


def rotary(values, positions):
    half_size = values.shape[-1] // 2
    freqs = 10000.0 ** (-2.0 * jnp.arange(half_size, dtype=jnp.float32) / values.shape[-1])
    angles = positions.astype(jnp.float32)[:, None] * freqs[None, :]
    cosine = jnp.cos(angles)[:, None, :]
    sine = jnp.sin(angles)[:, None, :]
    first_half = values[..., :half_size]
    second_half = values[..., half_size:]
    return jnp.concatenate(
        [first_half * cosine - second_half * sine, second_half * cosine + first_half * sine],
        axis=-1,
    )


def pair_swap(value):
    count = lax.axis_size("exp")
    return lax.ppermute(value, "exp", [(i, i ^ 1) for i in range(count)])


def merge_softmax(earlier, later):
    highest = jnp.maximum(earlier[0], later[0])
    return (
        highest,
        earlier[1] * jnp.exp(earlier[0] - highest) + later[1] * jnp.exp(later[0] - highest),
    )


def per_device(
    hidden,
    lengths,
    attn_gain,
    w_qkv,
    w_out,
    moe_gain,
    router,
    routes,
    w_gate_up,
    w_down,
    final_gain,
    lm_head,
):
    seq_count = lax.axis_size("seq")
    group_count = lax.axis_size("exp")
    device_count = seq_count * group_count
    token_rows = hidden[0]
    tok_rows = token_rows.shape[0]
    model_width = token_rows.shape[1]
    group_tokens = tok_rows * seq_count
    head_count = w_qkv.shape[2]
    head_size = w_qkv.shape[3]
    scale_factor = head_size ** (-0.5)
    prompt_lengths = lengths[0]
    segment, offset = segment_layout(prompt_lengths, group_tokens)
    normed = rms_scale(token_rows, attn_gain).astype(jnp.bfloat16)
    part_size = head_size // group_count
    own_part = lax.dynamic_slice_in_dim(
        w_out, lax.axis_index("exp") * part_size, part_size, axis=1
    )
    part_rows = own_part.shape[0] * part_size
    joined_rows = jnp.concatenate([normed, own_part.reshape(part_rows, model_width)], axis=0)
    gathered = lax.all_gather(joined_rows, "seq", axis=0)
    group_normed = gathered[:, :tok_rows].reshape(group_tokens, model_width)
    seq_part = gathered[:, tok_rows:].reshape((1, -1) + own_part.shape[1:])
    exp_index = lax.axis_index("exp")
    x_count = group_count // 2
    x_pieces, x_owners = [], []
    for step in range(1, x_count):
        x_pieces.append(
            lax.ppermute(
                seq_part[0],
                "exp",
                [(i, (i + 2 * step) % group_count) for i in range(group_count)],
            )
        )
        x_owners.append((exp_index - 2 * step) % group_count)
    qkv = jnp.einsum("td,dshe->tshe", group_normed, w_qkv, preferred_element_type=jnp.float32)
    query = rotary(qkv[:, 0], offset).astype(jnp.bfloat16)
    keys = rotary(qkv[:, 1], offset).astype(jnp.bfloat16)
    values = qkv[:, 2].astype(jnp.bfloat16)
    block_count = 4
    block_rows = group_tokens // block_count
    key_places = jnp.arange(group_tokens, dtype=jnp.int32)

    def one_block(block_index):
        first_row = block_index * block_rows
        key_count = first_row + block_rows
        block_query = query[first_row:key_count]
        block_segment = segment[first_row:key_count]
        query_places = key_places[first_row:key_count]
        scores = (
            jnp.einsum(
                "qhd,khd->hqk", block_query, keys[:key_count], preferred_element_type=jnp.float32
            )
            * scale_factor
        )
        allowed = (block_segment[:, None] == segment[None, :key_count]) & (
            key_places[None, :key_count] <= query_places[:, None]
        )
        scores = jnp.where(allowed[None], scores, -1e30)
        highest = jnp.max(scores, axis=2, keepdims=True)
        weights = jnp.exp(scores - highest)
        probs = (weights / jnp.sum(weights, axis=2, keepdims=True)).astype(jnp.bfloat16)
        return jnp.einsum(
            "hqk,khd->qhd", probs, values[:key_count], preferred_element_type=jnp.float32
        ).astype(jnp.bfloat16)

    blocks = jnp.concatenate([one_block(index) for index in range(block_count)], axis=0)
    x_pieces, blocks = lax.optimization_barrier((x_pieces, blocks))
    heads_flat = blocks.reshape(group_tokens, head_count * head_size)
    regrouped = lax.all_to_all(heads_flat, "seq", split_axis=0, concat_axis=1, tiled=True)
    pieces, owners = [seq_part[0]] + x_pieces, [exp_index] + x_owners
    partner_pieces = pair_swap(jnp.stack(pieces))
    pieces = pieces + [partner_pieces[step] for step in range(x_count)]
    owners = owners + [owner ^ 1 for owner in owners]
    regrouped = regrouped.reshape(tok_rows, -1, group_count, part_size)
    mixed = jnp.zeros((tok_rows, model_width), jnp.float32)
    for piece, owner in zip(pieces, owners):
        mixed = mixed + jnp.einsum(
            "thd,hdo->to",
            lax.dynamic_index_in_dim(regrouped, owner, axis=2, keepdims=False),
            piece,
            preferred_element_type=jnp.float32,
        )
    middle = (token_rows.astype(jnp.float32) + mixed).astype(jnp.bfloat16)
    expert_in = rms_scale(middle, moe_gain).astype(jnp.bfloat16)
    logits = jnp.dot(expert_in, router, preferred_element_type=jnp.float32)
    expert_count = router.shape[1]
    token_routes = routes[0]
    top_count = token_routes.shape[1]
    expert_ids = jnp.arange(expert_count, dtype=jnp.int32)
    chosen_mask = token_routes[:, :, None] == expert_ids[None, None, :]
    chosen = jnp.sum(jnp.where(chosen_mask, logits[:, None, :], 0.0), axis=2)
    gates = jax.nn.softmax(chosen, axis=-1)
    capacity = max(2, tok_rows * top_count * 7 // (6 * expert_count))
    flat_mask = chosen_mask.reshape(tok_rows * top_count, expert_count).astype(jnp.int32)
    earlier_count = jnp.cumsum(flat_mask, axis=0) - flat_mask
    slot_index = jnp.sum(earlier_count * flat_mask, axis=1)
    target = (token_routes.reshape(-1) * capacity + slot_index).reshape(tok_rows, top_count)
    slot_total = expert_count * capacity
    placed = target[:, :, None] == jnp.arange(slot_total, dtype=jnp.int32)[None, None, :]
    shares = device_count // expert_count
    assert capacity % shares == 0
    per_dest = capacity // shares
    dispatch_table = jnp.any(placed, axis=1).astype(jnp.bfloat16)
    dispatch_table = dispatch_table.reshape(tok_rows, device_count, per_dest)
    slot_weights = jnp.sum(jnp.where(placed, gates[:, :, None], 0.0), axis=1)
    slot_weights = slot_weights.reshape(tok_rows, device_count, per_dest)
    gate_up = w_gate_up[0]
    down_weight = w_down[0]
    other_gate_up = pair_swap(gate_up)
    other_down = pair_swap(down_weight)

    def share_part(rows, pair, down):
        both = jnp.einsum("scd,gfd->scgf", rows, pair, preferred_element_type=jnp.float32)
        act = (jax.nn.silu(both[:, :, 0]) * both[:, :, 1]).astype(jnp.bfloat16)
        part = jnp.einsum("scf,fd->scd", act, down, preferred_element_type=jnp.float32)
        return part.astype(jnp.bfloat16).astype(jnp.float32)

    cuts = [0, per_dest // 2, per_dest]
    routed = jnp.zeros((tok_rows, model_width), jnp.float32)
    for low, high in zip(cuts[:-1], cuts[1:]):
        outgoing = jnp.einsum(
            "tsc,tm->scm",
            dispatch_table[:, :, low:high],
            expert_in,
            preferred_element_type=jnp.float32,
        ).astype(jnp.bfloat16)
        arrived = lax.all_to_all(
            outgoing, ("seq", "exp"), split_axis=0, concat_axis=0, tiled=True
        )
        part_sum = share_part(arrived, gate_up, down_weight) + share_part(
            arrived, other_gate_up, other_down
        )
        returned = lax.all_to_all(
            part_sum.astype(jnp.bfloat16), ("seq", "exp"), split_axis=0, concat_axis=0, tiled=True
        )
        routed = routed + jnp.einsum(
            "tsc,scm->tm",
            slot_weights[:, :, low:high],
            returned.astype(jnp.float32),
            precision=lax.Precision.HIGHEST,
            preferred_element_type=jnp.float32,
        )
    layer_rows = (middle.astype(jnp.float32) + routed).astype(jnp.bfloat16)
    prompt_count = prompt_lengths.shape[0]
    last_places = jnp.cumsum(prompt_lengths) - 1
    here_places = lax.axis_index("seq") * tok_rows + jnp.arange(tok_rows, dtype=jnp.int32)
    select_table = (last_places[:, None] == here_places[None, :]).astype(jnp.bfloat16)
    picked = jnp.dot(select_table, layer_rows, preferred_element_type=jnp.float32)
    group_rows = lax.all_to_all(
        jnp.broadcast_to(
            picked.astype(jnp.bfloat16)[None], (seq_count, prompt_count, model_width)
        ),
        "seq",
        split_axis=0,
        concat_axis=0,
        tiled=True,
    )
    group_rows = jnp.sum(group_rows.astype(jnp.float32), axis=0).astype(jnp.bfloat16)
    last_rows = lax.all_to_all(
        jnp.broadcast_to(group_rows[None], (group_count, prompt_count, model_width)),
        "exp",
        split_axis=0,
        concat_axis=0,
        tiled=True,
    ).reshape(group_count * prompt_count, model_width).astype(jnp.float32)
    final = rms_scale(last_rows, final_gain).astype(jnp.bfloat16)
    vocab_scores = lax.dot_general(
        final, lm_head, (((1,), (1,)), ((), ())), preferred_element_type=jnp.float32
    )
    local_peak = jnp.max(vocab_scores, axis=1)
    local_total = jnp.sum(jnp.exp(vocab_scores - local_peak[:, None]), axis=1)
    local_stats = jnp.stack([local_peak, local_total])
    all_stats = lax.all_to_all(
        jnp.broadcast_to(local_stats[None], (device_count,) + local_stats.shape),
        ("seq", "exp"),
        split_axis=0,
        concat_axis=0,
        tiled=True,
    )
    all_peaks = all_stats[:, 0]
    global_peak = jnp.max(all_peaks, axis=0)
    global_total = jnp.sum(all_stats[:, 1] * jnp.exp(all_peaks - global_peak[None]), axis=0)
    logprobs = vocab_scores - (global_peak + jnp.log(global_total))[:, None]
    return (layer_rows[None], logprobs)


def solution(mesh):
    return jax.shard_map(
        per_device,
        mesh=mesh,
        in_specs=(
            P("exp", "seq", None),
            P("exp", None),
            P(),
            P(None, None, "seq", None),
            P("seq", None, None),
            P(),
            P(),
            P("exp", "seq", None),
            P(("seq", "exp"), None, None, None),
            P(("seq", "exp"), None, None),
            P(),
            P(("seq", "exp"), None),
        ),
        out_specs=(P("exp", "seq", None), P(None, ("seq", "exp"))),
        check_vma=False,
    )
```

```python
import jax
import jax.numpy as jnp
from jax import lax
from jax.sharding import PartitionSpec as P

epsilon = 1e-06


def joined(value, axis, join):
    pieces = jax.tree.map(lambda part: lax.all_gather(part, axis), value)
    head = jax.tree.map(lambda part: part[0], pieces)
    tail = jax.tree.map(lambda part: part[1:], pieces)
    subtotal, _ = lax.scan(lambda subtotal, piece: (join(subtotal, piece), None), head, tail)
    return subtotal


def rms_scale(values, gain):
    widened = values.astype(jnp.float32)
    inverse = lax.rsqrt(jnp.mean(widened * widened, axis=-1, keepdims=True) + epsilon)
    return widened * inverse * gain


def segment_layout(prompt_lengths, count):
    ends = jnp.cumsum(prompt_lengths)
    starts = ends - prompt_lengths
    places = jnp.arange(count, dtype=jnp.int32)
    member = ((places[:, None] >= starts[None, :]) & (places[:, None] < ends[None, :])).astype(
        jnp.int32
    )
    numbers = jnp.arange(prompt_lengths.shape[0], dtype=jnp.int32)
    segment = jnp.sum(member * numbers[None, :], axis=1)
    offset = places - jnp.sum(member * starts[None, :], axis=1)
    return (segment, offset)


def rotary(values, positions):
    half_size = values.shape[-1] // 2
    freqs = 10000.0 ** (-2.0 * jnp.arange(half_size, dtype=jnp.float32) / values.shape[-1])
    angles = positions.astype(jnp.float32)[:, None] * freqs[None, :]
    cosine = jnp.cos(angles)[:, None, :]
    sine = jnp.sin(angles)[:, None, :]
    first_half = values[..., :half_size]
    second_half = values[..., half_size:]
    return jnp.concatenate(
        [first_half * cosine - second_half * sine, second_half * cosine + first_half * sine],
        axis=-1,
    )


def pair_swap(value):
    count = lax.axis_size("exp")
    return lax.ppermute(value, "exp", [(i, i ^ 1) for i in range(count)])


def merge_softmax(earlier, later):
    highest = jnp.maximum(earlier[0], later[0])
    return (
        highest,
        earlier[1] * jnp.exp(earlier[0] - highest) + later[1] * jnp.exp(later[0] - highest),
    )


def per_device(
    hidden,
    lengths,
    attn_gain,
    w_qkv,
    w_out,
    moe_gain,
    router,
    routes,
    w_gate_up,
    w_down,
    final_gain,
    lm_head,
):
    seq_count = lax.axis_size("seq")
    group_count = lax.axis_size("exp")
    device_count = seq_count * group_count
    token_rows = hidden[0]
    tok_rows = token_rows.shape[0]
    model_width = token_rows.shape[1]
    group_tokens = tok_rows * seq_count
    head_count = w_qkv.shape[2]
    head_size = w_qkv.shape[3]
    scale_factor = head_size ** (-0.5)
    prompt_lengths = lengths[0]
    segment, offset = segment_layout(prompt_lengths, group_tokens)
    normed = rms_scale(token_rows, attn_gain).astype(jnp.bfloat16)
    group_normed = lax.all_gather(normed, "seq", axis=0, tiled=True)
    part_size = head_size // group_count
    own_part = lax.dynamic_slice_in_dim(
        w_out, lax.axis_index("exp") * part_size, part_size, axis=1
    )
    seq_part = lax.all_to_all(
        jnp.broadcast_to(own_part[None], (seq_count,) + own_part.shape),
        "seq",
        split_axis=0,
        concat_axis=0,
        tiled=True,
    ).reshape((1, -1) + own_part.shape[1:])
    exp_index = lax.axis_index("exp")
    x_count = group_count // 2
    x_pieces, x_owners = [], []
    for step in range(1, x_count):
        x_pieces.append(
            lax.ppermute(
                seq_part[0],
                "exp",
                [(i, (i + 2 * step) % group_count) for i in range(group_count)],
            )
        )
        x_owners.append((exp_index - 2 * step) % group_count)
    qkv = jnp.einsum("td,dshe->tshe", group_normed, w_qkv, preferred_element_type=jnp.float32)
    query = rotary(qkv[:, 0], offset).astype(jnp.bfloat16)
    keys = rotary(qkv[:, 1], offset).astype(jnp.bfloat16)
    values = qkv[:, 2].astype(jnp.bfloat16)
    block_count = 4
    block_rows = group_tokens // block_count
    key_places = jnp.arange(group_tokens, dtype=jnp.int32)

    def one_block(block_index):
        first_row = block_index * block_rows
        key_count = first_row + block_rows
        block_query = query[first_row:key_count]
        block_segment = segment[first_row:key_count]
        query_places = key_places[first_row:key_count]
        scores = (
            jnp.einsum(
                "qhd,khd->hqk", block_query, keys[:key_count], preferred_element_type=jnp.float32
            )
            * scale_factor
        )
        allowed = (block_segment[:, None] == segment[None, :key_count]) & (
            key_places[None, :key_count] <= query_places[:, None]
        )
        scores = jnp.where(allowed[None], scores, -1e30)
        highest = jnp.max(scores, axis=2, keepdims=True)
        weights = jnp.exp(scores - highest)
        probs = (weights / jnp.sum(weights, axis=2, keepdims=True)).astype(jnp.bfloat16)
        return jnp.einsum(
            "hqk,khd->qhd", probs, values[:key_count], preferred_element_type=jnp.float32
        ).astype(jnp.bfloat16)

    blocks = jnp.concatenate([one_block(index) for index in range(block_count)], axis=0)
    x_pieces, blocks = lax.optimization_barrier((x_pieces, blocks))
    heads_flat = blocks.reshape(group_tokens, head_count * head_size)
    regrouped = lax.all_to_all(heads_flat, "seq", split_axis=0, concat_axis=1, tiled=True)
    pieces, owners = [seq_part[0]] + x_pieces, [exp_index] + x_owners
    pieces = pieces + [pair_swap(piece) for piece in pieces]
    owners = owners + [owner ^ 1 for owner in owners]
    regrouped = regrouped.reshape(tok_rows, -1, group_count, part_size)
    mixed = jnp.zeros((tok_rows, model_width), jnp.float32)
    for piece, owner in zip(pieces, owners):
        mixed = mixed + jnp.einsum(
            "thd,hdo->to",
            lax.dynamic_index_in_dim(regrouped, owner, axis=2, keepdims=False),
            piece,
            preferred_element_type=jnp.float32,
        )
    middle = (token_rows.astype(jnp.float32) + mixed).astype(jnp.bfloat16)
    expert_in = rms_scale(middle, moe_gain).astype(jnp.bfloat16)
    logits = jnp.dot(expert_in, router, preferred_element_type=jnp.float32)
    expert_count = router.shape[1]
    token_routes = routes[0]
    top_count = token_routes.shape[1]
    expert_ids = jnp.arange(expert_count, dtype=jnp.int32)
    chosen_mask = token_routes[:, :, None] == expert_ids[None, None, :]
    chosen = jnp.sum(jnp.where(chosen_mask, logits[:, None, :], 0.0), axis=2)
    gates = jax.nn.softmax(chosen, axis=-1)
    capacity = max(2, tok_rows * top_count * 7 // (6 * expert_count))
    flat_mask = chosen_mask.reshape(tok_rows * top_count, expert_count).astype(jnp.int32)
    earlier_count = jnp.cumsum(flat_mask, axis=0) - flat_mask
    slot_index = jnp.sum(earlier_count * flat_mask, axis=1)
    target = (token_routes.reshape(-1) * capacity + slot_index).reshape(tok_rows, top_count)
    slot_total = expert_count * capacity
    placed = target[:, :, None] == jnp.arange(slot_total, dtype=jnp.int32)[None, None, :]
    shares = device_count // expert_count
    assert capacity % shares == 0
    per_dest = capacity // shares
    dispatch_table = jnp.any(placed, axis=1).astype(jnp.bfloat16)
    dispatch_table = dispatch_table.reshape(tok_rows, device_count, per_dest)
    slot_weights = jnp.sum(jnp.where(placed, gates[:, :, None], 0.0), axis=1)
    slot_weights = slot_weights.reshape(tok_rows, device_count, per_dest)
    gate_up = w_gate_up[0]
    down_weight = w_down[0]
    other_gate_up = pair_swap(gate_up)
    other_down = pair_swap(down_weight)

    def share_part(rows, pair, down):
        both = jnp.einsum("scd,gfd->scgf", rows, pair, preferred_element_type=jnp.float32)
        act = (jax.nn.silu(both[:, :, 0]) * both[:, :, 1]).astype(jnp.bfloat16)
        part = jnp.einsum("scf,fd->scd", act, down, preferred_element_type=jnp.float32)
        return part.astype(jnp.bfloat16).astype(jnp.float32)

    cuts = [0, per_dest // 2, per_dest]
    routed = jnp.zeros((tok_rows, model_width), jnp.float32)
    for low, high in zip(cuts[:-1], cuts[1:]):
        outgoing = jnp.einsum(
            "tsc,tm->scm",
            dispatch_table[:, :, low:high],
            expert_in,
            preferred_element_type=jnp.float32,
        ).astype(jnp.bfloat16)
        arrived = lax.all_to_all(
            outgoing, ("seq", "exp"), split_axis=0, concat_axis=0, tiled=True
        )
        part_sum = share_part(arrived, gate_up, down_weight) + share_part(
            arrived, other_gate_up, other_down
        )
        returned = lax.all_to_all(
            part_sum.astype(jnp.bfloat16), ("seq", "exp"), split_axis=0, concat_axis=0, tiled=True
        )
        routed = routed + jnp.einsum(
            "tsc,scm->tm",
            slot_weights[:, :, low:high],
            returned.astype(jnp.float32),
            precision=lax.Precision.HIGHEST,
            preferred_element_type=jnp.float32,
        )
    layer_rows = (middle.astype(jnp.float32) + routed).astype(jnp.bfloat16)
    prompt_count = prompt_lengths.shape[0]
    last_places = jnp.cumsum(prompt_lengths) - 1
    here_places = lax.axis_index("seq") * tok_rows + jnp.arange(tok_rows, dtype=jnp.int32)
    select_table = (last_places[:, None] == here_places[None, :]).astype(jnp.bfloat16)
    picked = jnp.dot(select_table, layer_rows, preferred_element_type=jnp.float32)
    group_rows = lax.all_to_all(
        jnp.broadcast_to(
            picked.astype(jnp.bfloat16)[None], (seq_count, prompt_count, model_width)
        ),
        "seq",
        split_axis=0,
        concat_axis=0,
        tiled=True,
    )
    group_rows = jnp.sum(group_rows.astype(jnp.float32), axis=0).astype(jnp.bfloat16)
    last_rows = lax.all_to_all(
        jnp.broadcast_to(group_rows[None], (group_count, prompt_count, model_width)),
        "exp",
        split_axis=0,
        concat_axis=0,
        tiled=True,
    ).reshape(group_count * prompt_count, model_width).astype(jnp.float32)
    final = rms_scale(last_rows, final_gain).astype(jnp.bfloat16)
    vocab_scores = lax.dot_general(
        final, lm_head, (((1,), (1,)), ((), ())), preferred_element_type=jnp.float32
    )
    local_peak = jnp.max(vocab_scores, axis=1)
    local_total = jnp.sum(jnp.exp(vocab_scores - local_peak[:, None]), axis=1)
    local_stats = jnp.stack([local_peak, local_total])
    all_stats = lax.all_to_all(
        jnp.broadcast_to(local_stats[None], (device_count,) + local_stats.shape),
        ("seq", "exp"),
        split_axis=0,
        concat_axis=0,
        tiled=True,
    )
    all_peaks = all_stats[:, 0]
    global_peak = jnp.max(all_peaks, axis=0)
    global_total = jnp.sum(all_stats[:, 1] * jnp.exp(all_peaks - global_peak[None]), axis=0)
    logprobs = vocab_scores - (global_peak + jnp.log(global_total))[:, None]
    return (layer_rows[None], logprobs)


def solution(mesh):
    return jax.shard_map(
        per_device,
        mesh=mesh,
        in_specs=(
            P("exp", "seq", None),
            P("exp", None),
            P(),
            P(None, None, "seq", None),
            P("seq", None, None),
            P(),
            P(),
            P("exp", "seq", None),
            P(("seq", "exp"), None, None, None),
            P(("seq", "exp"), None, None),
            P(),
            P(("seq", "exp"), None),
        ),
        out_specs=(P("exp", "seq", None), P(None, ("seq", "exp"))),
        check_vma=False,
    )
```

```python
import jax
import jax.numpy as jnp
from jax import lax
from jax.sharding import PartitionSpec as P

epsilon = 1e-06


def joined(value, axis, join):
    pieces = jax.tree.map(lambda part: lax.all_gather(part, axis), value)
    head = jax.tree.map(lambda part: part[0], pieces)
    tail = jax.tree.map(lambda part: part[1:], pieces)
    subtotal, _ = lax.scan(lambda subtotal, piece: (join(subtotal, piece), None), head, tail)
    return subtotal


def rms_scale(values, gain):
    widened = values.astype(jnp.float32)
    inverse = lax.rsqrt(jnp.mean(widened * widened, axis=-1, keepdims=True) + epsilon)
    return widened * inverse * gain


def segment_layout(prompt_lengths, count):
    ends = jnp.cumsum(prompt_lengths)
    starts = ends - prompt_lengths
    places = jnp.arange(count, dtype=jnp.int32)
    member = ((places[:, None] >= starts[None, :]) & (places[:, None] < ends[None, :])).astype(
        jnp.int32
    )
    numbers = jnp.arange(prompt_lengths.shape[0], dtype=jnp.int32)
    segment = jnp.sum(member * numbers[None, :], axis=1)
    offset = places - jnp.sum(member * starts[None, :], axis=1)
    return (segment, offset)


def rotary(values, positions):
    half_size = values.shape[-1] // 2
    freqs = 10000.0 ** (-2.0 * jnp.arange(half_size, dtype=jnp.float32) / values.shape[-1])
    angles = positions.astype(jnp.float32)[:, None] * freqs[None, :]
    cosine = jnp.cos(angles)[:, None, :]
    sine = jnp.sin(angles)[:, None, :]
    first_half = values[..., :half_size]
    second_half = values[..., half_size:]
    return jnp.concatenate(
        [first_half * cosine - second_half * sine, second_half * cosine + first_half * sine],
        axis=-1,
    )


def pair_swap(value):
    count = lax.axis_size("exp")
    return lax.ppermute(value, "exp", [(i, i ^ 1) for i in range(count)])


def merge_softmax(earlier, later):
    highest = jnp.maximum(earlier[0], later[0])
    return (
        highest,
        earlier[1] * jnp.exp(earlier[0] - highest) + later[1] * jnp.exp(later[0] - highest),
    )


def per_device(
    hidden,
    lengths,
    attn_gain,
    w_qkv,
    w_out,
    moe_gain,
    router,
    routes,
    w_gate_up,
    w_down,
    final_gain,
    lm_head,
):
    seq_count = lax.axis_size("seq")
    group_count = lax.axis_size("exp")
    device_count = seq_count * group_count
    token_rows = hidden[0]
    tok_rows = token_rows.shape[0]
    model_width = token_rows.shape[1]
    group_tokens = tok_rows * seq_count
    head_count = w_qkv.shape[2]
    head_size = w_qkv.shape[3]
    scale_factor = head_size ** (-0.5)
    prompt_lengths = lengths[0]
    segment, offset = segment_layout(prompt_lengths, group_tokens)
    normed = rms_scale(token_rows, attn_gain).astype(jnp.bfloat16)
    group_normed = lax.all_gather(normed, "seq", axis=0, tiled=True)
    part_size = head_size // group_count
    own_part = lax.dynamic_slice_in_dim(
        w_out, lax.axis_index("exp") * part_size, part_size, axis=1
    )
    seq_part = lax.all_to_all(
        jnp.broadcast_to(own_part[None], (seq_count,) + own_part.shape),
        "seq",
        split_axis=0,
        concat_axis=0,
        tiled=True,
    ).reshape((1, -1) + own_part.shape[1:])
    exp_index = lax.axis_index("exp")
    x_count = group_count // 2
    x_pieces, x_owners = [], []
    for step in range(1, x_count):
        x_pieces.append(
            lax.ppermute(
                seq_part[0],
                "exp",
                [(i, (i + 2 * step) % group_count) for i in range(group_count)],
            )
        )
        x_owners.append((exp_index - 2 * step) % group_count)
    qkv = jnp.einsum("td,dshe->tshe", group_normed, w_qkv, preferred_element_type=jnp.float32)
    query = rotary(qkv[:, 0], offset).astype(jnp.bfloat16)
    keys = rotary(qkv[:, 1], offset).astype(jnp.bfloat16)
    values = qkv[:, 2].astype(jnp.bfloat16)
    block_count = 4
    block_rows = group_tokens // block_count
    key_places = jnp.arange(group_tokens, dtype=jnp.int32)

    def one_block(block_index):
        first_row = block_index * block_rows
        key_count = first_row + block_rows
        block_query = query[first_row:key_count]
        block_segment = segment[first_row:key_count]
        query_places = key_places[first_row:key_count]
        scores = (
            jnp.einsum(
                "qhd,khd->hqk", block_query, keys[:key_count], preferred_element_type=jnp.float32
            )
            * scale_factor
        )
        allowed = (block_segment[:, None] == segment[None, :key_count]) & (
            key_places[None, :key_count] <= query_places[:, None]
        )
        scores = jnp.where(allowed[None], scores, -1e30)
        highest = jnp.max(scores, axis=2, keepdims=True)
        weights = jnp.exp(scores - highest)
        probs = (weights / jnp.sum(weights, axis=2, keepdims=True)).astype(jnp.bfloat16)
        return jnp.einsum(
            "hqk,khd->qhd", probs, values[:key_count], preferred_element_type=jnp.float32
        ).astype(jnp.bfloat16)

    blocks = jnp.concatenate([one_block(index) for index in range(block_count)], axis=0)
    x_pieces, blocks = lax.optimization_barrier((x_pieces, blocks))
    heads_flat = blocks.reshape(group_tokens, head_count * head_size)
    regrouped = lax.all_to_all(heads_flat, "seq", split_axis=0, concat_axis=1, tiled=True)
    pieces, owners = [seq_part[0]] + x_pieces, [exp_index] + x_owners
    pieces = pieces + [pair_swap(piece) for piece in pieces]
    owners = owners + [owner ^ 1 for owner in owners]
    regrouped = regrouped.reshape(tok_rows, -1, group_count, part_size)
    mixed = jnp.zeros((tok_rows, model_width), jnp.float32)
    for piece, owner in zip(pieces, owners):
        mixed = mixed + jnp.einsum(
            "thd,hdo->to",
            lax.dynamic_index_in_dim(regrouped, owner, axis=2, keepdims=False),
            piece,
            preferred_element_type=jnp.float32,
        )
    middle = (token_rows.astype(jnp.float32) + mixed).astype(jnp.bfloat16)
    expert_in = rms_scale(middle, moe_gain).astype(jnp.bfloat16)
    logits = jnp.dot(expert_in, router, preferred_element_type=jnp.float32)
    expert_count = router.shape[1]
    token_routes = routes[0]
    top_count = token_routes.shape[1]
    expert_ids = jnp.arange(expert_count, dtype=jnp.int32)
    chosen_mask = token_routes[:, :, None] == expert_ids[None, None, :]
    chosen = jnp.sum(jnp.where(chosen_mask, logits[:, None, :], 0.0), axis=2)
    gates = jax.nn.softmax(chosen, axis=-1)
    capacity = max(2, tok_rows * top_count * 7 // (6 * expert_count))
    flat_mask = chosen_mask.reshape(tok_rows * top_count, expert_count).astype(jnp.int32)
    earlier_count = jnp.cumsum(flat_mask, axis=0) - flat_mask
    slot_index = jnp.sum(earlier_count * flat_mask, axis=1)
    target = (token_routes.reshape(-1) * capacity + slot_index).reshape(tok_rows, top_count)
    slot_total = expert_count * capacity
    placed = target[:, :, None] == jnp.arange(slot_total, dtype=jnp.int32)[None, None, :]
    shares = device_count // expert_count
    assert capacity % shares == 0
    per_dest = capacity // shares
    dispatch_table = jnp.any(placed, axis=1).astype(jnp.bfloat16)
    dispatch_table = dispatch_table.reshape(tok_rows, device_count, per_dest)
    slot_weights = jnp.sum(jnp.where(placed, gates[:, :, None], 0.0), axis=1)
    slot_weights = slot_weights.reshape(tok_rows, device_count, per_dest)
    gate_up = w_gate_up[0]
    down_weight = w_down[0]
    other_gate_up = pair_swap(gate_up)
    other_down = pair_swap(down_weight)

    def share_part(rows, pair, down):
        both = jnp.einsum("scd,gfd->scgf", rows, pair, preferred_element_type=jnp.float32)
        act = (jax.nn.silu(both[:, :, 0]) * both[:, :, 1]).astype(jnp.bfloat16)
        part = jnp.einsum("scf,fd->scd", act, down, preferred_element_type=jnp.float32)
        return part.astype(jnp.bfloat16).astype(jnp.float32)

    first_cut = 16 if per_dest > 16 else per_dest // 2
    cuts = [0, first_cut, per_dest]
    routed = jnp.zeros((tok_rows, model_width), jnp.float32)
    for low, high in zip(cuts[:-1], cuts[1:]):
        outgoing = jnp.einsum(
            "tsc,tm->scm",
            dispatch_table[:, :, low:high],
            expert_in,
            preferred_element_type=jnp.float32,
        ).astype(jnp.bfloat16)
        arrived = lax.all_to_all(
            outgoing, ("seq", "exp"), split_axis=0, concat_axis=0, tiled=True
        )
        part_sum = share_part(arrived, gate_up, down_weight) + share_part(
            arrived, other_gate_up, other_down
        )
        returned = lax.all_to_all(
            part_sum.astype(jnp.bfloat16), ("seq", "exp"), split_axis=0, concat_axis=0, tiled=True
        )
        routed = routed + jnp.einsum(
            "tsc,scm->tm",
            slot_weights[:, :, low:high],
            returned.astype(jnp.float32),
            precision=lax.Precision.HIGHEST,
            preferred_element_type=jnp.float32,
        )
    layer_rows = (middle.astype(jnp.float32) + routed).astype(jnp.bfloat16)
    prompt_count = prompt_lengths.shape[0]
    last_places = jnp.cumsum(prompt_lengths) - 1
    here_places = lax.axis_index("seq") * tok_rows + jnp.arange(tok_rows, dtype=jnp.int32)
    select_table = (last_places[:, None] == here_places[None, :]).astype(jnp.bfloat16)
    picked = jnp.dot(select_table, layer_rows, preferred_element_type=jnp.float32)
    group_rows = lax.all_to_all(
        jnp.broadcast_to(
            picked.astype(jnp.bfloat16)[None], (seq_count, prompt_count, model_width)
        ),
        "seq",
        split_axis=0,
        concat_axis=0,
        tiled=True,
    )
    group_rows = jnp.sum(group_rows.astype(jnp.float32), axis=0).astype(jnp.bfloat16)
    last_rows = lax.all_to_all(
        jnp.broadcast_to(group_rows[None], (group_count, prompt_count, model_width)),
        "exp",
        split_axis=0,
        concat_axis=0,
        tiled=True,
    ).reshape(group_count * prompt_count, model_width).astype(jnp.float32)
    final = rms_scale(last_rows, final_gain).astype(jnp.bfloat16)
    vocab_scores = lax.dot_general(
        final, lm_head, (((1,), (1,)), ((), ())), preferred_element_type=jnp.float32
    )
    local_peak = jnp.max(vocab_scores, axis=1)
    local_total = jnp.sum(jnp.exp(vocab_scores - local_peak[:, None]), axis=1)
    local_stats = jnp.stack([local_peak, local_total])
    all_stats = lax.all_to_all(
        jnp.broadcast_to(local_stats[None], (device_count,) + local_stats.shape),
        ("seq", "exp"),
        split_axis=0,
        concat_axis=0,
        tiled=True,
    )
    all_peaks = all_stats[:, 0]
    global_peak = jnp.max(all_peaks, axis=0)
    global_total = jnp.sum(all_stats[:, 1] * jnp.exp(all_peaks - global_peak[None]), axis=0)
    logprobs = vocab_scores - (global_peak + jnp.log(global_total))[:, None]
    return (layer_rows[None], logprobs)


def solution(mesh):
    return jax.shard_map(
        per_device,
        mesh=mesh,
        in_specs=(
            P("exp", "seq", None),
            P("exp", None),
            P(),
            P(None, None, "seq", None),
            P("seq", None, None),
            P(),
            P(),
            P("exp", "seq", None),
            P(("seq", "exp"), None, None, None),
            P(("seq", "exp"), None, None),
            P(),
            P(("seq", "exp"), None),
        ),
        out_specs=(P("exp", "seq", None), P(None, ("seq", "exp"))),
        check_vma=False,
    )
```

```python
import jax
import jax.numpy as jnp
from jax import lax
from jax.sharding import PartitionSpec as P

epsilon = 1e-06


def joined(value, axis, join):
    pieces = jax.tree.map(lambda part: lax.all_gather(part, axis), value)
    head = jax.tree.map(lambda part: part[0], pieces)
    tail = jax.tree.map(lambda part: part[1:], pieces)
    subtotal, _ = lax.scan(lambda subtotal, piece: (join(subtotal, piece), None), head, tail)
    return subtotal


def rms_scale(values, gain):
    widened = values.astype(jnp.float32)
    inverse = lax.rsqrt(jnp.mean(widened * widened, axis=-1, keepdims=True) + epsilon)
    return widened * inverse * gain


def segment_layout(prompt_lengths, count):
    ends = jnp.cumsum(prompt_lengths)
    starts = ends - prompt_lengths
    places = jnp.arange(count, dtype=jnp.int32)
    member = ((places[:, None] >= starts[None, :]) & (places[:, None] < ends[None, :])).astype(
        jnp.int32
    )
    numbers = jnp.arange(prompt_lengths.shape[0], dtype=jnp.int32)
    segment = jnp.sum(member * numbers[None, :], axis=1)
    offset = places - jnp.sum(member * starts[None, :], axis=1)
    return (segment, offset)


def rotary(values, positions):
    half_size = values.shape[-1] // 2
    freqs = 10000.0 ** (-2.0 * jnp.arange(half_size, dtype=jnp.float32) / values.shape[-1])
    angles = positions.astype(jnp.float32)[:, None] * freqs[None, :]
    cosine = jnp.cos(angles)[:, None, :]
    sine = jnp.sin(angles)[:, None, :]
    first_half = values[..., :half_size]
    second_half = values[..., half_size:]
    return jnp.concatenate(
        [first_half * cosine - second_half * sine, second_half * cosine + first_half * sine],
        axis=-1,
    )


def pair_swap(value):
    count = lax.axis_size("exp")
    return lax.ppermute(value, "exp", [(i, i ^ 1) for i in range(count)])


def merge_softmax(earlier, later):
    highest = jnp.maximum(earlier[0], later[0])
    return (
        highest,
        earlier[1] * jnp.exp(earlier[0] - highest) + later[1] * jnp.exp(later[0] - highest),
    )


def per_device(
    hidden,
    lengths,
    attn_gain,
    w_qkv,
    w_out,
    moe_gain,
    router,
    routes,
    w_gate_up,
    w_down,
    final_gain,
    lm_head,
):
    seq_count = lax.axis_size("seq")
    group_count = lax.axis_size("exp")
    device_count = seq_count * group_count
    token_rows = hidden[0]
    tok_rows = token_rows.shape[0]
    model_width = token_rows.shape[1]
    group_tokens = tok_rows * seq_count
    head_count = w_qkv.shape[2]
    head_size = w_qkv.shape[3]
    scale_factor = head_size ** (-0.5)
    prompt_lengths = lengths[0]
    segment, offset = segment_layout(prompt_lengths, group_tokens)
    normed = rms_scale(token_rows, attn_gain).astype(jnp.bfloat16)
    group_normed = lax.all_gather(normed, "seq", axis=0, tiled=True)
    gate_up = w_gate_up[0]
    down_weight = w_down[0]
    other_gate_up = pair_swap(gate_up)
    other_down = pair_swap(down_weight)
    other_gate_up, other_down, group_normed = lax.optimization_barrier(
        (other_gate_up, other_down, group_normed)
    )
    part_size = head_size // group_count
    own_part = lax.dynamic_slice_in_dim(
        w_out, lax.axis_index("exp") * part_size, part_size, axis=1
    )
    seq_part = lax.all_to_all(
        jnp.broadcast_to(own_part[None], (seq_count,) + own_part.shape),
        "seq",
        split_axis=0,
        concat_axis=0,
        tiled=True,
    ).reshape((1, -1) + own_part.shape[1:])
    exp_index = lax.axis_index("exp")
    x_count = group_count // 2
    x_pieces, x_owners = [], []
    for step in range(1, x_count):
        x_pieces.append(
            lax.ppermute(
                seq_part[0],
                "exp",
                [(i, (i + 2 * step) % group_count) for i in range(group_count)],
            )
        )
        x_owners.append((exp_index - 2 * step) % group_count)
    qkv = jnp.einsum("td,dshe->tshe", group_normed, w_qkv, preferred_element_type=jnp.float32)
    query = rotary(qkv[:, 0], offset).astype(jnp.bfloat16)
    keys = rotary(qkv[:, 1], offset).astype(jnp.bfloat16)
    values = qkv[:, 2].astype(jnp.bfloat16)
    block_count = 4
    block_rows = group_tokens // block_count
    key_places = jnp.arange(group_tokens, dtype=jnp.int32)

    def one_block(block_index):
        first_row = block_index * block_rows
        key_count = first_row + block_rows
        block_query = query[first_row:key_count]
        block_segment = segment[first_row:key_count]
        query_places = key_places[first_row:key_count]
        scores = (
            jnp.einsum(
                "qhd,khd->hqk", block_query, keys[:key_count], preferred_element_type=jnp.float32
            )
            * scale_factor
        )
        allowed = (block_segment[:, None] == segment[None, :key_count]) & (
            key_places[None, :key_count] <= query_places[:, None]
        )
        scores = jnp.where(allowed[None], scores, -1e30)
        highest = jnp.max(scores, axis=2, keepdims=True)
        weights = jnp.exp(scores - highest)
        probs = (weights / jnp.sum(weights, axis=2, keepdims=True)).astype(jnp.bfloat16)
        return jnp.einsum(
            "hqk,khd->qhd", probs, values[:key_count], preferred_element_type=jnp.float32
        ).astype(jnp.bfloat16)

    blocks = jnp.concatenate([one_block(index) for index in range(block_count)], axis=0)
    x_pieces, blocks = lax.optimization_barrier((x_pieces, blocks))
    heads_flat = blocks.reshape(group_tokens, head_count * head_size)
    regrouped = lax.all_to_all(heads_flat, "seq", split_axis=0, concat_axis=1, tiled=True)
    pieces, owners = [seq_part[0]] + x_pieces, [exp_index] + x_owners
    pieces = pieces + [pair_swap(piece) for piece in pieces]
    owners = owners + [owner ^ 1 for owner in owners]
    regrouped = regrouped.reshape(tok_rows, -1, group_count, part_size)
    mixed = jnp.zeros((tok_rows, model_width), jnp.float32)
    for piece, owner in zip(pieces, owners):
        mixed = mixed + jnp.einsum(
            "thd,hdo->to",
            lax.dynamic_index_in_dim(regrouped, owner, axis=2, keepdims=False),
            piece,
            preferred_element_type=jnp.float32,
        )
    middle = (token_rows.astype(jnp.float32) + mixed).astype(jnp.bfloat16)
    expert_in = rms_scale(middle, moe_gain).astype(jnp.bfloat16)
    logits = jnp.dot(expert_in, router, preferred_element_type=jnp.float32)
    expert_count = router.shape[1]
    token_routes = routes[0]
    top_count = token_routes.shape[1]
    expert_ids = jnp.arange(expert_count, dtype=jnp.int32)
    chosen_mask = token_routes[:, :, None] == expert_ids[None, None, :]
    chosen = jnp.sum(jnp.where(chosen_mask, logits[:, None, :], 0.0), axis=2)
    gates = jax.nn.softmax(chosen, axis=-1)
    capacity = max(2, tok_rows * top_count * 7 // (6 * expert_count))
    flat_mask = chosen_mask.reshape(tok_rows * top_count, expert_count).astype(jnp.int32)
    earlier_count = jnp.cumsum(flat_mask, axis=0) - flat_mask
    slot_index = jnp.sum(earlier_count * flat_mask, axis=1)
    target = (token_routes.reshape(-1) * capacity + slot_index).reshape(tok_rows, top_count)
    slot_total = expert_count * capacity
    placed = target[:, :, None] == jnp.arange(slot_total, dtype=jnp.int32)[None, None, :]
    shares = device_count // expert_count
    assert capacity % shares == 0
    per_dest = capacity // shares
    dispatch_table = jnp.any(placed, axis=1).astype(jnp.bfloat16)
    dispatch_table = dispatch_table.reshape(tok_rows, device_count, per_dest)
    slot_weights = jnp.sum(jnp.where(placed, gates[:, :, None], 0.0), axis=1)
    slot_weights = slot_weights.reshape(tok_rows, device_count, per_dest)

    def share_part(rows, pair, down):
        both = jnp.einsum("scd,gfd->scgf", rows, pair, preferred_element_type=jnp.float32)
        act = (jax.nn.silu(both[:, :, 0]) * both[:, :, 1]).astype(jnp.bfloat16)
        part = jnp.einsum("scf,fd->scd", act, down, preferred_element_type=jnp.float32)
        return part.astype(jnp.bfloat16).astype(jnp.float32)

    cuts = [0, per_dest // 2, per_dest]
    routed = jnp.zeros((tok_rows, model_width), jnp.float32)
    for low, high in zip(cuts[:-1], cuts[1:]):
        outgoing = jnp.einsum(
            "tsc,tm->scm",
            dispatch_table[:, :, low:high],
            expert_in,
            preferred_element_type=jnp.float32,
        ).astype(jnp.bfloat16)
        arrived = lax.all_to_all(
            outgoing, ("seq", "exp"), split_axis=0, concat_axis=0, tiled=True
        )
        part_sum = share_part(arrived, gate_up, down_weight) + share_part(
            arrived, other_gate_up, other_down
        )
        returned = lax.all_to_all(
            part_sum.astype(jnp.bfloat16), ("seq", "exp"), split_axis=0, concat_axis=0, tiled=True
        )
        routed = routed + jnp.einsum(
            "tsc,scm->tm",
            slot_weights[:, :, low:high],
            returned.astype(jnp.float32),
            precision=lax.Precision.HIGHEST,
            preferred_element_type=jnp.float32,
        )
    layer_rows = (middle.astype(jnp.float32) + routed).astype(jnp.bfloat16)
    prompt_count = prompt_lengths.shape[0]
    last_places = jnp.cumsum(prompt_lengths) - 1
    here_places = lax.axis_index("seq") * tok_rows + jnp.arange(tok_rows, dtype=jnp.int32)
    select_table = (last_places[:, None] == here_places[None, :]).astype(jnp.bfloat16)
    picked = jnp.dot(select_table, layer_rows, preferred_element_type=jnp.float32)
    group_rows = lax.all_to_all(
        jnp.broadcast_to(
            picked.astype(jnp.bfloat16)[None], (seq_count, prompt_count, model_width)
        ),
        "seq",
        split_axis=0,
        concat_axis=0,
        tiled=True,
    )
    group_rows = jnp.sum(group_rows.astype(jnp.float32), axis=0).astype(jnp.bfloat16)
    last_rows = lax.all_to_all(
        jnp.broadcast_to(group_rows[None], (group_count, prompt_count, model_width)),
        "exp",
        split_axis=0,
        concat_axis=0,
        tiled=True,
    ).reshape(group_count * prompt_count, model_width).astype(jnp.float32)
    final = rms_scale(last_rows, final_gain).astype(jnp.bfloat16)
    vocab_scores = lax.dot_general(
        final, lm_head, (((1,), (1,)), ((), ())), preferred_element_type=jnp.float32
    )
    local_peak = jnp.max(vocab_scores, axis=1)
    local_total = jnp.sum(jnp.exp(vocab_scores - local_peak[:, None]), axis=1)
    local_stats = jnp.stack([local_peak, local_total])
    all_stats = lax.all_to_all(
        jnp.broadcast_to(local_stats[None], (device_count,) + local_stats.shape),
        ("seq", "exp"),
        split_axis=0,
        concat_axis=0,
        tiled=True,
    )
    all_peaks = all_stats[:, 0]
    global_peak = jnp.max(all_peaks, axis=0)
    global_total = jnp.sum(all_stats[:, 1] * jnp.exp(all_peaks - global_peak[None]), axis=0)
    logprobs = vocab_scores - (global_peak + jnp.log(global_total))[:, None]
    return (layer_rows[None], logprobs)


def solution(mesh):
    return jax.shard_map(
        per_device,
        mesh=mesh,
        in_specs=(
            P("exp", "seq", None),
            P("exp", None),
            P(),
            P(None, None, "seq", None),
            P("seq", None, None),
            P(),
            P(),
            P("exp", "seq", None),
            P(("seq", "exp"), None, None, None),
            P(("seq", "exp"), None, None),
            P(),
            P(("seq", "exp"), None),
        ),
        out_specs=(P("exp", "seq", None), P(None, ("seq", "exp"))),
        check_vma=False,
    )
```

```python
import jax
import jax.numpy as jnp
from jax import lax
from jax.sharding import PartitionSpec as P

epsilon = 1e-06


def joined(value, axis, join):
    pieces = jax.tree.map(lambda part: lax.all_gather(part, axis), value)
    head = jax.tree.map(lambda part: part[0], pieces)
    tail = jax.tree.map(lambda part: part[1:], pieces)
    subtotal, _ = lax.scan(lambda subtotal, piece: (join(subtotal, piece), None), head, tail)
    return subtotal


def rms_scale(values, gain):
    widened = values.astype(jnp.float32)
    inverse = lax.rsqrt(jnp.mean(widened * widened, axis=-1, keepdims=True) + epsilon)
    return widened * inverse * gain


def segment_layout(prompt_lengths, count):
    ends = jnp.cumsum(prompt_lengths)
    starts = ends - prompt_lengths
    places = jnp.arange(count, dtype=jnp.int32)
    member = ((places[:, None] >= starts[None, :]) & (places[:, None] < ends[None, :])).astype(
        jnp.int32
    )
    numbers = jnp.arange(prompt_lengths.shape[0], dtype=jnp.int32)
    segment = jnp.sum(member * numbers[None, :], axis=1)
    offset = places - jnp.sum(member * starts[None, :], axis=1)
    return (segment, offset)


def rotary(values, positions):
    half_size = values.shape[-1] // 2
    freqs = 10000.0 ** (-2.0 * jnp.arange(half_size, dtype=jnp.float32) / values.shape[-1])
    angles = positions.astype(jnp.float32)[:, None] * freqs[None, :]
    cosine = jnp.cos(angles)[:, None, :]
    sine = jnp.sin(angles)[:, None, :]
    first_half = values[..., :half_size]
    second_half = values[..., half_size:]
    return jnp.concatenate(
        [first_half * cosine - second_half * sine, second_half * cosine + first_half * sine],
        axis=-1,
    )


def pair_swap(value):
    count = lax.axis_size("exp")
    return lax.ppermute(value, "exp", [(i, i ^ 1) for i in range(count)])


def merge_softmax(earlier, later):
    highest = jnp.maximum(earlier[0], later[0])
    return (
        highest,
        earlier[1] * jnp.exp(earlier[0] - highest) + later[1] * jnp.exp(later[0] - highest),
    )


def per_device(
    hidden,
    lengths,
    attn_gain,
    w_qkv,
    w_out,
    moe_gain,
    router,
    routes,
    w_gate_up,
    w_down,
    final_gain,
    lm_head,
):
    seq_count = lax.axis_size("seq")
    group_count = lax.axis_size("exp")
    device_count = seq_count * group_count
    token_rows = hidden[0]
    tok_rows = token_rows.shape[0]
    model_width = token_rows.shape[1]
    group_tokens = tok_rows * seq_count
    head_count = w_qkv.shape[2]
    head_size = w_qkv.shape[3]
    scale_factor = head_size ** (-0.5)
    prompt_lengths = lengths[0]
    segment, offset = segment_layout(prompt_lengths, group_tokens)
    normed = rms_scale(token_rows, attn_gain).astype(jnp.bfloat16)
    group_normed = lax.all_gather(normed, "seq", axis=0, tiled=True)
    gate_up = w_gate_up[0]
    down_weight = w_down[0]
    other_gate_up = pair_swap(gate_up)
    other_down = pair_swap(down_weight)
    other_gate_up, other_down, group_normed = lax.optimization_barrier(
        (other_gate_up, other_down, group_normed)
    )
    part_size = head_size // group_count
    own_part = lax.dynamic_slice_in_dim(
        w_out, lax.axis_index("exp") * part_size, part_size, axis=1
    )
    seq_part = lax.all_to_all(
        jnp.broadcast_to(own_part[None], (seq_count,) + own_part.shape),
        "seq",
        split_axis=0,
        concat_axis=0,
        tiled=True,
    ).reshape((1, -1) + own_part.shape[1:])
    exp_index = lax.axis_index("exp")
    x_count = group_count // 2
    x_pieces, x_owners = [], []
    for step in range(1, x_count):
        x_pieces.append(
            lax.ppermute(
                seq_part[0],
                "exp",
                [(i, (i + 2 * step) % group_count) for i in range(group_count)],
            )
        )
        x_owners.append((exp_index - 2 * step) % group_count)
    qkv = jnp.einsum("td,dshe->tshe", group_normed, w_qkv, preferred_element_type=jnp.float32)
    query = rotary(qkv[:, 0], offset).astype(jnp.bfloat16)
    keys = rotary(qkv[:, 1], offset).astype(jnp.bfloat16)
    values = qkv[:, 2].astype(jnp.bfloat16)
    block_count = 4
    block_rows = group_tokens // block_count
    key_places = jnp.arange(group_tokens, dtype=jnp.int32)

    def one_block(block_index):
        first_row = block_index * block_rows
        key_count = first_row + block_rows
        block_query = query[first_row:key_count]
        block_segment = segment[first_row:key_count]
        query_places = key_places[first_row:key_count]
        scores = (
            jnp.einsum(
                "qhd,khd->hqk", block_query, keys[:key_count], preferred_element_type=jnp.float32
            )
            * scale_factor
        )
        allowed = (block_segment[:, None] == segment[None, :key_count]) & (
            key_places[None, :key_count] <= query_places[:, None]
        )
        scores = jnp.where(allowed[None], scores, -1e30)
        highest = jnp.max(scores, axis=2, keepdims=True)
        weights = jnp.exp(scores - highest)
        probs = (weights / jnp.sum(weights, axis=2, keepdims=True)).astype(jnp.bfloat16)
        return jnp.einsum(
            "hqk,khd->qhd", probs, values[:key_count], preferred_element_type=jnp.float32
        ).astype(jnp.bfloat16)

    blocks = jnp.concatenate([one_block(index) for index in range(block_count)], axis=0)
    heads_flat = blocks.reshape(group_tokens, head_count * head_size)
    regrouped = lax.all_to_all(heads_flat, "seq", split_axis=0, concat_axis=1, tiled=True)
    x_pieces, regrouped = lax.optimization_barrier((x_pieces, regrouped))
    pieces, owners = [seq_part[0]] + x_pieces, [exp_index] + x_owners
    pieces = pieces + [pair_swap(piece) for piece in pieces]
    owners = owners + [owner ^ 1 for owner in owners]
    regrouped = regrouped.reshape(tok_rows, -1, group_count, part_size)
    mixed = jnp.zeros((tok_rows, model_width), jnp.float32)
    for piece, owner in zip(pieces, owners):
        mixed = mixed + jnp.einsum(
            "thd,hdo->to",
            lax.dynamic_index_in_dim(regrouped, owner, axis=2, keepdims=False),
            piece,
            preferred_element_type=jnp.float32,
        )
    middle = (token_rows.astype(jnp.float32) + mixed).astype(jnp.bfloat16)
    expert_in = rms_scale(middle, moe_gain).astype(jnp.bfloat16)
    logits = jnp.dot(expert_in, router, preferred_element_type=jnp.float32)
    expert_count = router.shape[1]
    token_routes = routes[0]
    top_count = token_routes.shape[1]
    expert_ids = jnp.arange(expert_count, dtype=jnp.int32)
    chosen_mask = token_routes[:, :, None] == expert_ids[None, None, :]
    chosen = jnp.sum(jnp.where(chosen_mask, logits[:, None, :], 0.0), axis=2)
    gates = jax.nn.softmax(chosen, axis=-1)
    capacity = max(2, tok_rows * top_count * 7 // (6 * expert_count))
    flat_mask = chosen_mask.reshape(tok_rows * top_count, expert_count).astype(jnp.int32)
    earlier_count = jnp.cumsum(flat_mask, axis=0) - flat_mask
    slot_index = jnp.sum(earlier_count * flat_mask, axis=1)
    target = (token_routes.reshape(-1) * capacity + slot_index).reshape(tok_rows, top_count)
    slot_total = expert_count * capacity
    placed = target[:, :, None] == jnp.arange(slot_total, dtype=jnp.int32)[None, None, :]
    shares = device_count // expert_count
    assert capacity % shares == 0
    per_dest = capacity // shares
    dispatch_table = jnp.any(placed, axis=1).astype(jnp.bfloat16)
    dispatch_table = dispatch_table.reshape(tok_rows, device_count, per_dest)
    slot_weights = jnp.sum(jnp.where(placed, gates[:, :, None], 0.0), axis=1)
    slot_weights = slot_weights.reshape(tok_rows, device_count, per_dest)

    def share_part(rows, pair, down):
        both = jnp.einsum("scd,gfd->scgf", rows, pair, preferred_element_type=jnp.float32)
        act = (jax.nn.silu(both[:, :, 0]) * both[:, :, 1]).astype(jnp.bfloat16)
        part = jnp.einsum("scf,fd->scd", act, down, preferred_element_type=jnp.float32)
        return part.astype(jnp.bfloat16).astype(jnp.float32)

    cuts = [0, per_dest // 2, per_dest]
    routed = jnp.zeros((tok_rows, model_width), jnp.float32)
    for low, high in zip(cuts[:-1], cuts[1:]):
        outgoing = jnp.einsum(
            "tsc,tm->scm",
            dispatch_table[:, :, low:high],
            expert_in,
            preferred_element_type=jnp.float32,
        ).astype(jnp.bfloat16)
        arrived = lax.all_to_all(
            outgoing, ("seq", "exp"), split_axis=0, concat_axis=0, tiled=True
        )
        part_sum = share_part(arrived, gate_up, down_weight) + share_part(
            arrived, other_gate_up, other_down
        )
        returned = lax.all_to_all(
            part_sum.astype(jnp.bfloat16), ("seq", "exp"), split_axis=0, concat_axis=0, tiled=True
        )
        routed = routed + jnp.einsum(
            "tsc,scm->tm",
            slot_weights[:, :, low:high],
            returned.astype(jnp.float32),
            precision=lax.Precision.HIGHEST,
            preferred_element_type=jnp.float32,
        )
    layer_rows = (middle.astype(jnp.float32) + routed).astype(jnp.bfloat16)
    prompt_count = prompt_lengths.shape[0]
    last_places = jnp.cumsum(prompt_lengths) - 1
    here_places = lax.axis_index("seq") * tok_rows + jnp.arange(tok_rows, dtype=jnp.int32)
    select_table = (last_places[:, None] == here_places[None, :]).astype(jnp.bfloat16)
    picked = jnp.dot(select_table, layer_rows, preferred_element_type=jnp.float32)
    group_rows = lax.all_to_all(
        jnp.broadcast_to(
            picked.astype(jnp.bfloat16)[None], (seq_count, prompt_count, model_width)
        ),
        "seq",
        split_axis=0,
        concat_axis=0,
        tiled=True,
    )
    group_rows = jnp.sum(group_rows.astype(jnp.float32), axis=0).astype(jnp.bfloat16)
    last_rows = lax.all_to_all(
        jnp.broadcast_to(group_rows[None], (group_count, prompt_count, model_width)),
        "exp",
        split_axis=0,
        concat_axis=0,
        tiled=True,
    ).reshape(group_count * prompt_count, model_width).astype(jnp.float32)
    final = rms_scale(last_rows, final_gain).astype(jnp.bfloat16)
    vocab_scores = lax.dot_general(
        final, lm_head, (((1,), (1,)), ((), ())), preferred_element_type=jnp.float32
    )
    local_peak = jnp.max(vocab_scores, axis=1)
    local_total = jnp.sum(jnp.exp(vocab_scores - local_peak[:, None]), axis=1)
    local_stats = jnp.stack([local_peak, local_total])
    all_stats = lax.all_to_all(
        jnp.broadcast_to(local_stats[None], (device_count,) + local_stats.shape),
        ("seq", "exp"),
        split_axis=0,
        concat_axis=0,
        tiled=True,
    )
    all_peaks = all_stats[:, 0]
    global_peak = jnp.max(all_peaks, axis=0)
    global_total = jnp.sum(all_stats[:, 1] * jnp.exp(all_peaks - global_peak[None]), axis=0)
    logprobs = vocab_scores - (global_peak + jnp.log(global_total))[:, None]
    return (layer_rows[None], logprobs)


def solution(mesh):
    return jax.shard_map(
        per_device,
        mesh=mesh,
        in_specs=(
            P("exp", "seq", None),
            P("exp", None),
            P(),
            P(None, None, "seq", None),
            P("seq", None, None),
            P(),
            P(),
            P("exp", "seq", None),
            P(("seq", "exp"), None, None, None),
            P(("seq", "exp"), None, None),
            P(),
            P(("seq", "exp"), None),
        ),
        out_specs=(P("exp", "seq", None), P(None, ("seq", "exp"))),
        check_vma=False,
    )
```

```python
import jax
import jax.numpy as jnp
from jax import lax
from jax.sharding import PartitionSpec as P

epsilon = 1e-06


def joined(value, axis, join):
    pieces = jax.tree.map(lambda part: lax.all_gather(part, axis), value)
    head = jax.tree.map(lambda part: part[0], pieces)
    tail = jax.tree.map(lambda part: part[1:], pieces)
    subtotal, _ = lax.scan(lambda subtotal, piece: (join(subtotal, piece), None), head, tail)
    return subtotal


def rms_scale(values, gain):
    widened = values.astype(jnp.float32)
    inverse = lax.rsqrt(jnp.mean(widened * widened, axis=-1, keepdims=True) + epsilon)
    return widened * inverse * gain


def segment_layout(prompt_lengths, count):
    ends = jnp.cumsum(prompt_lengths)
    starts = ends - prompt_lengths
    places = jnp.arange(count, dtype=jnp.int32)
    member = ((places[:, None] >= starts[None, :]) & (places[:, None] < ends[None, :])).astype(
        jnp.int32
    )
    numbers = jnp.arange(prompt_lengths.shape[0], dtype=jnp.int32)
    segment = jnp.sum(member * numbers[None, :], axis=1)
    offset = places - jnp.sum(member * starts[None, :], axis=1)
    return (segment, offset)


def rotary(values, positions):
    half_size = values.shape[-1] // 2
    freqs = 10000.0 ** (-2.0 * jnp.arange(half_size, dtype=jnp.float32) / values.shape[-1])
    angles = positions.astype(jnp.float32)[:, None] * freqs[None, :]
    cosine = jnp.cos(angles)[:, None, :]
    sine = jnp.sin(angles)[:, None, :]
    first_half = values[..., :half_size]
    second_half = values[..., half_size:]
    return jnp.concatenate(
        [first_half * cosine - second_half * sine, second_half * cosine + first_half * sine],
        axis=-1,
    )


def pair_swap(value):
    count = lax.axis_size("exp")
    return lax.ppermute(value, "exp", [(i, i ^ 1) for i in range(count)])


def merge_softmax(earlier, later):
    highest = jnp.maximum(earlier[0], later[0])
    return (
        highest,
        earlier[1] * jnp.exp(earlier[0] - highest) + later[1] * jnp.exp(later[0] - highest),
    )


def per_device(
    hidden,
    lengths,
    attn_gain,
    w_qkv,
    w_out,
    moe_gain,
    router,
    routes,
    w_gate_up,
    w_down,
    final_gain,
    lm_head,
):
    seq_count = lax.axis_size("seq")
    group_count = lax.axis_size("exp")
    device_count = seq_count * group_count
    token_rows = hidden[0]
    tok_rows = token_rows.shape[0]
    model_width = token_rows.shape[1]
    group_tokens = tok_rows * seq_count
    head_count = w_qkv.shape[2]
    head_size = w_qkv.shape[3]
    scale_factor = head_size ** (-0.5)
    prompt_lengths = lengths[0]
    segment, offset = segment_layout(prompt_lengths, group_tokens)
    normed = rms_scale(token_rows, attn_gain).astype(jnp.bfloat16)
    group_normed = lax.all_gather(normed, "seq", axis=0, tiled=True)
    gate_up = w_gate_up[0]
    down_weight = w_down[0]
    other_gate_up = pair_swap(gate_up)
    other_down = pair_swap(down_weight)
    early_flat = (
        routes[0].reshape(-1, 1) == jnp.arange(router.shape[1], dtype=jnp.int32)[None, :]
    ).astype(jnp.int32)
    early_count = jnp.cumsum(early_flat, axis=0) - early_flat
    early_slots = jnp.sum(early_count * early_flat, axis=1)
    other_gate_up, other_down, early_slots, group_normed = lax.optimization_barrier(
        (other_gate_up, other_down, early_slots, group_normed)
    )
    part_size = head_size // group_count
    own_part = lax.dynamic_slice_in_dim(
        w_out, lax.axis_index("exp") * part_size, part_size, axis=1
    )
    seq_part = lax.all_to_all(
        jnp.broadcast_to(own_part[None], (seq_count,) + own_part.shape),
        "seq",
        split_axis=0,
        concat_axis=0,
        tiled=True,
    ).reshape((1, -1) + own_part.shape[1:])
    exp_index = lax.axis_index("exp")
    x_count = group_count // 2
    x_pieces, x_owners = [], []
    for step in range(1, x_count):
        x_pieces.append(
            lax.ppermute(
                seq_part[0],
                "exp",
                [(i, (i + 2 * step) % group_count) for i in range(group_count)],
            )
        )
        x_owners.append((exp_index - 2 * step) % group_count)
    qkv = jnp.einsum("td,dshe->tshe", group_normed, w_qkv, preferred_element_type=jnp.float32)
    query = rotary(qkv[:, 0], offset).astype(jnp.bfloat16)
    keys = rotary(qkv[:, 1], offset).astype(jnp.bfloat16)
    values = qkv[:, 2].astype(jnp.bfloat16)
    block_count = 4
    block_rows = group_tokens // block_count
    key_places = jnp.arange(group_tokens, dtype=jnp.int32)

    def one_block(block_index):
        first_row = block_index * block_rows
        key_count = first_row + block_rows
        block_query = query[first_row:key_count]
        block_segment = segment[first_row:key_count]
        query_places = key_places[first_row:key_count]
        scores = (
            jnp.einsum(
                "qhd,khd->hqk", block_query, keys[:key_count], preferred_element_type=jnp.float32
            )
            * scale_factor
        )
        allowed = (block_segment[:, None] == segment[None, :key_count]) & (
            key_places[None, :key_count] <= query_places[:, None]
        )
        scores = jnp.where(allowed[None], scores, -1e30)
        highest = jnp.max(scores, axis=2, keepdims=True)
        weights = jnp.exp(scores - highest)
        probs = (weights / jnp.sum(weights, axis=2, keepdims=True)).astype(jnp.bfloat16)
        return jnp.einsum(
            "hqk,khd->qhd", probs, values[:key_count], preferred_element_type=jnp.float32
        ).astype(jnp.bfloat16)

    blocks = jnp.concatenate([one_block(index) for index in range(block_count)], axis=0)
    heads_flat = blocks.reshape(group_tokens, head_count * head_size)
    regrouped = lax.all_to_all(heads_flat, "seq", split_axis=0, concat_axis=1, tiled=True)
    x_pieces, regrouped = lax.optimization_barrier((x_pieces, regrouped))
    pieces, owners = [seq_part[0]] + x_pieces, [exp_index] + x_owners
    pieces = pieces + [pair_swap(piece) for piece in pieces]
    owners = owners + [owner ^ 1 for owner in owners]
    regrouped = regrouped.reshape(tok_rows, -1, group_count, part_size)
    mixed = jnp.zeros((tok_rows, model_width), jnp.float32)
    for piece, owner in zip(pieces, owners):
        mixed = mixed + jnp.einsum(
            "thd,hdo->to",
            lax.dynamic_index_in_dim(regrouped, owner, axis=2, keepdims=False),
            piece,
            preferred_element_type=jnp.float32,
        )
    middle = (token_rows.astype(jnp.float32) + mixed).astype(jnp.bfloat16)
    expert_in = rms_scale(middle, moe_gain).astype(jnp.bfloat16)
    logits = jnp.dot(expert_in, router, preferred_element_type=jnp.float32)
    expert_count = router.shape[1]
    token_routes = routes[0]
    top_count = token_routes.shape[1]
    expert_ids = jnp.arange(expert_count, dtype=jnp.int32)
    chosen_mask = token_routes[:, :, None] == expert_ids[None, None, :]
    chosen = jnp.sum(jnp.where(chosen_mask, logits[:, None, :], 0.0), axis=2)
    gates = jax.nn.softmax(chosen, axis=-1)
    capacity = max(2, tok_rows * top_count * 7 // (6 * expert_count))
    slot_index = early_slots
    target = (token_routes.reshape(-1) * capacity + slot_index).reshape(tok_rows, top_count)
    target, chosen_mask = lax.optimization_barrier((target, chosen_mask))
    slot_total = expert_count * capacity
    placed = target[:, :, None] == jnp.arange(slot_total, dtype=jnp.int32)[None, None, :]
    shares = device_count // expert_count
    assert capacity % shares == 0
    per_dest = capacity // shares
    dispatch_table = jnp.any(placed, axis=1).astype(jnp.bfloat16)
    dispatch_table = dispatch_table.reshape(tok_rows, device_count, per_dest)
    slot_weights = jnp.sum(jnp.where(placed, gates[:, :, None], 0.0), axis=1)
    slot_weights = slot_weights.reshape(tok_rows, device_count, per_dest)

    def share_part(rows, pair, down):
        both = jnp.einsum("scd,gfd->scgf", rows, pair, preferred_element_type=jnp.float32)
        act = (jax.nn.silu(both[:, :, 0]) * both[:, :, 1]).astype(jnp.bfloat16)
        part = jnp.einsum("scf,fd->scd", act, down, preferred_element_type=jnp.float32)
        return part.astype(jnp.bfloat16).astype(jnp.float32)

    cuts = [0, per_dest // 2, per_dest]
    routed = jnp.zeros((tok_rows, model_width), jnp.float32)
    for low, high in zip(cuts[:-1], cuts[1:]):
        outgoing = jnp.einsum(
            "tsc,tm->scm",
            dispatch_table[:, :, low:high],
            expert_in,
            preferred_element_type=jnp.float32,
        ).astype(jnp.bfloat16)
        arrived = lax.all_to_all(
            outgoing, ("seq", "exp"), split_axis=0, concat_axis=0, tiled=True
        )
        part_sum = share_part(arrived, gate_up, down_weight) + share_part(
            arrived, other_gate_up, other_down
        )
        returned = lax.all_to_all(
            part_sum.astype(jnp.bfloat16), ("seq", "exp"), split_axis=0, concat_axis=0, tiled=True
        )
        routed = routed + jnp.einsum(
            "tsc,scm->tm",
            slot_weights[:, :, low:high],
            returned.astype(jnp.float32),
            precision=lax.Precision.HIGHEST,
            preferred_element_type=jnp.float32,
        )
    layer_rows = (middle.astype(jnp.float32) + routed).astype(jnp.bfloat16)
    prompt_count = prompt_lengths.shape[0]
    last_places = jnp.cumsum(prompt_lengths) - 1
    here_places = lax.axis_index("seq") * tok_rows + jnp.arange(tok_rows, dtype=jnp.int32)
    select_table = (last_places[:, None] == here_places[None, :]).astype(jnp.bfloat16)
    picked = jnp.dot(select_table, layer_rows, preferred_element_type=jnp.float32)
    group_rows = lax.all_to_all(
        jnp.broadcast_to(
            picked.astype(jnp.bfloat16)[None], (seq_count, prompt_count, model_width)
        ),
        "seq",
        split_axis=0,
        concat_axis=0,
        tiled=True,
    )
    group_rows = jnp.sum(group_rows.astype(jnp.float32), axis=0).astype(jnp.bfloat16)
    last_rows = lax.all_to_all(
        jnp.broadcast_to(group_rows[None], (group_count, prompt_count, model_width)),
        "exp",
        split_axis=0,
        concat_axis=0,
        tiled=True,
    ).reshape(group_count * prompt_count, model_width).astype(jnp.float32)
    final = rms_scale(last_rows, final_gain).astype(jnp.bfloat16)
    vocab_scores = lax.dot_general(
        final, lm_head, (((1,), (1,)), ((), ())), preferred_element_type=jnp.float32
    )
    local_peak = jnp.max(vocab_scores, axis=1)
    local_total = jnp.sum(jnp.exp(vocab_scores - local_peak[:, None]), axis=1)
    local_stats = jnp.stack([local_peak, local_total])
    all_stats = lax.all_to_all(
        jnp.broadcast_to(local_stats[None], (device_count,) + local_stats.shape),
        ("seq", "exp"),
        split_axis=0,
        concat_axis=0,
        tiled=True,
    )
    all_peaks = all_stats[:, 0]
    global_peak = jnp.max(all_peaks, axis=0)
    global_total = jnp.sum(all_stats[:, 1] * jnp.exp(all_peaks - global_peak[None]), axis=0)
    logprobs = vocab_scores - (global_peak + jnp.log(global_total))[:, None]
    return (layer_rows[None], logprobs)


def solution(mesh):
    return jax.shard_map(
        per_device,
        mesh=mesh,
        in_specs=(
            P("exp", "seq", None),
            P("exp", None),
            P(),
            P(None, None, "seq", None),
            P("seq", None, None),
            P(),
            P(),
            P("exp", "seq", None),
            P(("seq", "exp"), None, None, None),
            P(("seq", "exp"), None, None),
            P(),
            P(("seq", "exp"), None),
        ),
        out_specs=(P("exp", "seq", None), P(None, ("seq", "exp"))),
        check_vma=False,
    )
```

```python
import jax
import jax.numpy as jnp
from jax import lax
from jax.sharding import PartitionSpec as P

epsilon = 1e-06


def joined(value, axis, join):
    pieces = jax.tree.map(lambda part: lax.all_gather(part, axis), value)
    head = jax.tree.map(lambda part: part[0], pieces)
    tail = jax.tree.map(lambda part: part[1:], pieces)
    subtotal, _ = lax.scan(lambda subtotal, piece: (join(subtotal, piece), None), head, tail)
    return subtotal


def rms_scale(values, gain):
    widened = values.astype(jnp.float32)
    inverse = lax.rsqrt(jnp.mean(widened * widened, axis=-1, keepdims=True) + epsilon)
    return widened * inverse * gain


def segment_layout(prompt_lengths, count):
    ends = jnp.cumsum(prompt_lengths)
    starts = ends - prompt_lengths
    places = jnp.arange(count, dtype=jnp.int32)
    member = ((places[:, None] >= starts[None, :]) & (places[:, None] < ends[None, :])).astype(
        jnp.int32
    )
    numbers = jnp.arange(prompt_lengths.shape[0], dtype=jnp.int32)
    segment = jnp.sum(member * numbers[None, :], axis=1)
    offset = places - jnp.sum(member * starts[None, :], axis=1)
    return (segment, offset)


def rotary(values, positions):
    half_size = values.shape[-1] // 2
    freqs = 10000.0 ** (-2.0 * jnp.arange(half_size, dtype=jnp.float32) / values.shape[-1])
    angles = positions.astype(jnp.float32)[:, None] * freqs[None, :]
    cosine = jnp.cos(angles)[:, None, :]
    sine = jnp.sin(angles)[:, None, :]
    first_half = values[..., :half_size]
    second_half = values[..., half_size:]
    return jnp.concatenate(
        [first_half * cosine - second_half * sine, second_half * cosine + first_half * sine],
        axis=-1,
    )


def pair_swap(value):
    count = lax.axis_size("exp")
    return lax.ppermute(value, "exp", [(i, i ^ 1) for i in range(count)])


def merge_softmax(earlier, later):
    highest = jnp.maximum(earlier[0], later[0])
    return (
        highest,
        earlier[1] * jnp.exp(earlier[0] - highest) + later[1] * jnp.exp(later[0] - highest),
    )


def per_device(
    hidden,
    lengths,
    attn_gain,
    w_qkv,
    w_out,
    moe_gain,
    router,
    routes,
    w_gate_up,
    w_down,
    final_gain,
    lm_head,
):
    seq_count = lax.axis_size("seq")
    group_count = lax.axis_size("exp")
    device_count = seq_count * group_count
    token_rows = hidden[0]
    tok_rows = token_rows.shape[0]
    model_width = token_rows.shape[1]
    group_tokens = tok_rows * seq_count
    head_count = w_qkv.shape[2]
    head_size = w_qkv.shape[3]
    scale_factor = head_size ** (-0.5)
    prompt_lengths = lengths[0]
    segment, offset = segment_layout(prompt_lengths, group_tokens)
    normed = rms_scale(token_rows, attn_gain).astype(jnp.bfloat16)
    group_normed = lax.all_gather(normed, "seq", axis=0, tiled=True)
    gate_up = w_gate_up[0]
    down_weight = w_down[0]
    other_gate_up = pair_swap(gate_up)
    other_down = pair_swap(down_weight)
    other_gate_up, other_down, group_normed = lax.optimization_barrier(
        (other_gate_up, other_down, group_normed)
    )
    part_size = head_size // group_count
    own_part = lax.dynamic_slice_in_dim(
        w_out, lax.axis_index("exp") * part_size, part_size, axis=1
    )
    seq_part = lax.all_to_all(
        jnp.broadcast_to(own_part[None], (seq_count,) + own_part.shape),
        "seq",
        split_axis=0,
        concat_axis=0,
        tiled=True,
    ).reshape((1, -1) + own_part.shape[1:])
    exp_index = lax.axis_index("exp")
    x_count = group_count // 2
    x_pieces, x_owners = [], []
    for step in range(1, x_count):
        x_pieces.append(
            lax.ppermute(
                seq_part[0],
                "exp",
                [(i, (i + 2 * step) % group_count) for i in range(group_count)],
            )
        )
        x_owners.append((exp_index - 2 * step) % group_count)
    qkv = jnp.einsum("td,dshe->tshe", group_normed, w_qkv, preferred_element_type=jnp.float32)
    query = rotary(qkv[:, 0], offset).astype(jnp.bfloat16)
    keys = rotary(qkv[:, 1], offset).astype(jnp.bfloat16)
    values = qkv[:, 2].astype(jnp.bfloat16)
    block_count = 4
    block_rows = group_tokens // block_count
    key_places = jnp.arange(group_tokens, dtype=jnp.int32)

    def one_block(block_index):
        first_row = block_index * block_rows
        key_count = first_row + block_rows
        block_query = query[first_row:key_count]
        block_segment = segment[first_row:key_count]
        query_places = key_places[first_row:key_count]
        scores = (
            jnp.einsum(
                "qhd,khd->hqk", block_query, keys[:key_count], preferred_element_type=jnp.float32
            )
            * scale_factor
        )
        allowed = (block_segment[:, None] == segment[None, :key_count]) & (
            key_places[None, :key_count] <= query_places[:, None]
        )
        scores = jnp.where(allowed[None], scores, -1e30)
        highest = jnp.max(scores, axis=2, keepdims=True)
        weights = jnp.exp(scores - highest)
        probs = (weights / jnp.sum(weights, axis=2, keepdims=True)).astype(jnp.bfloat16)
        return jnp.einsum(
            "hqk,khd->qhd", probs, values[:key_count], preferred_element_type=jnp.float32
        ).astype(jnp.bfloat16)

    blocks = jnp.concatenate([one_block(index) for index in range(block_count)], axis=0)
    heads_flat = blocks.reshape(group_tokens, head_count * head_size)
    regrouped = lax.all_to_all(heads_flat, "seq", split_axis=0, concat_axis=1, tiled=True)
    x_pieces, regrouped = lax.optimization_barrier((x_pieces, regrouped))
    pieces, owners = [seq_part[0]] + x_pieces, [exp_index] + x_owners
    pieces = pieces + [pair_swap(piece) for piece in pieces]
    owners = owners + [owner ^ 1 for owner in owners]
    regrouped = regrouped.reshape(tok_rows, -1, group_count, part_size)
    mixed = jnp.zeros((tok_rows, model_width), jnp.float32)
    for piece, owner in zip(pieces, owners):
        mixed = mixed + jnp.einsum(
            "thd,hdo->to",
            lax.dynamic_index_in_dim(regrouped, owner, axis=2, keepdims=False),
            piece,
            preferred_element_type=jnp.float32,
        )
    middle = (token_rows.astype(jnp.float32) + mixed).astype(jnp.bfloat16)
    expert_in = rms_scale(middle, moe_gain).astype(jnp.bfloat16)
    logits = jnp.dot(expert_in, router, preferred_element_type=jnp.float32)
    expert_count = router.shape[1]
    token_routes = routes[0]
    top_count = token_routes.shape[1]
    expert_ids = jnp.arange(expert_count, dtype=jnp.int32)
    chosen_mask = token_routes[:, :, None] == expert_ids[None, None, :]
    chosen = jnp.sum(jnp.where(chosen_mask, logits[:, None, :], 0.0), axis=2)
    gates = jax.nn.softmax(chosen, axis=-1)
    capacity = max(2, tok_rows * top_count * 7 // (6 * expert_count))
    flat_mask = chosen_mask.reshape(tok_rows * top_count, expert_count).astype(jnp.int32)
    earlier_count = jnp.cumsum(flat_mask, axis=0) - flat_mask
    slot_index = jnp.sum(earlier_count * flat_mask, axis=1)
    target = (token_routes.reshape(-1) * capacity + slot_index).reshape(tok_rows, top_count)
    slot_total = expert_count * capacity
    placed = target[:, :, None] == jnp.arange(slot_total, dtype=jnp.int32)[None, None, :]
    shares = device_count // expert_count
    assert capacity % shares == 0
    per_dest = capacity // shares
    dispatch_table = jnp.any(placed, axis=1).astype(jnp.bfloat16)
    dispatch_table = dispatch_table.reshape(tok_rows, device_count, per_dest)
    slot_weights = jnp.sum(jnp.where(placed, gates[:, :, None], 0.0), axis=1)
    slot_weights = slot_weights.reshape(tok_rows, device_count, per_dest)

    def share_part(rows, pair, down):
        both = jnp.einsum("scd,gfd->scgf", rows, pair, preferred_element_type=jnp.float32)
        act = (jax.nn.silu(both[:, :, 0]) * both[:, :, 1]).astype(jnp.bfloat16)
        part = jnp.einsum("scf,fd->scd", act, down, preferred_element_type=jnp.float32)
        return part.astype(jnp.bfloat16).astype(jnp.float32)

    first_cut = per_dest - 16 if per_dest > 16 else per_dest // 2
    cuts = [0, first_cut, per_dest]
    routed = jnp.zeros((tok_rows, model_width), jnp.float32)
    for low, high in zip(cuts[:-1], cuts[1:]):
        outgoing = jnp.einsum(
            "tsc,tm->scm",
            dispatch_table[:, :, low:high],
            expert_in,
            preferred_element_type=jnp.float32,
        ).astype(jnp.bfloat16)
        arrived = lax.all_to_all(
            outgoing, ("seq", "exp"), split_axis=0, concat_axis=0, tiled=True
        )
        part_sum = share_part(arrived, gate_up, down_weight) + share_part(
            arrived, other_gate_up, other_down
        )
        returned = lax.all_to_all(
            part_sum.astype(jnp.bfloat16), ("seq", "exp"), split_axis=0, concat_axis=0, tiled=True
        )
        routed = routed + jnp.einsum(
            "tsc,scm->tm",
            slot_weights[:, :, low:high],
            returned.astype(jnp.float32),
            precision=lax.Precision.HIGHEST,
            preferred_element_type=jnp.float32,
        )
    layer_rows = (middle.astype(jnp.float32) + routed).astype(jnp.bfloat16)
    prompt_count = prompt_lengths.shape[0]
    last_places = jnp.cumsum(prompt_lengths) - 1
    here_places = lax.axis_index("seq") * tok_rows + jnp.arange(tok_rows, dtype=jnp.int32)
    select_table = (last_places[:, None] == here_places[None, :]).astype(jnp.bfloat16)
    picked = jnp.dot(select_table, layer_rows, preferred_element_type=jnp.float32)
    group_rows = lax.all_to_all(
        jnp.broadcast_to(
            picked.astype(jnp.bfloat16)[None], (seq_count, prompt_count, model_width)
        ),
        "seq",
        split_axis=0,
        concat_axis=0,
        tiled=True,
    )
    group_rows = jnp.sum(group_rows.astype(jnp.float32), axis=0).astype(jnp.bfloat16)
    last_rows = lax.all_to_all(
        jnp.broadcast_to(group_rows[None], (group_count, prompt_count, model_width)),
        "exp",
        split_axis=0,
        concat_axis=0,
        tiled=True,
    ).reshape(group_count * prompt_count, model_width).astype(jnp.float32)
    final = rms_scale(last_rows, final_gain).astype(jnp.bfloat16)
    vocab_scores = lax.dot_general(
        final, lm_head, (((1,), (1,)), ((), ())), preferred_element_type=jnp.float32
    )
    local_peak = jnp.max(vocab_scores, axis=1)
    local_total = jnp.sum(jnp.exp(vocab_scores - local_peak[:, None]), axis=1)
    local_stats = jnp.stack([local_peak, local_total])
    all_stats = lax.all_to_all(
        jnp.broadcast_to(local_stats[None], (device_count,) + local_stats.shape),
        ("seq", "exp"),
        split_axis=0,
        concat_axis=0,
        tiled=True,
    )
    all_peaks = all_stats[:, 0]
    global_peak = jnp.max(all_peaks, axis=0)
    global_total = jnp.sum(all_stats[:, 1] * jnp.exp(all_peaks - global_peak[None]), axis=0)
    logprobs = vocab_scores - (global_peak + jnp.log(global_total))[:, None]
    return (layer_rows[None], logprobs)


def solution(mesh):
    return jax.shard_map(
        per_device,
        mesh=mesh,
        in_specs=(
            P("exp", "seq", None),
            P("exp", None),
            P(),
            P(None, None, "seq", None),
            P("seq", None, None),
            P(),
            P(),
            P("exp", "seq", None),
            P(("seq", "exp"), None, None, None),
            P(("seq", "exp"), None, None),
            P(),
            P(("seq", "exp"), None),
        ),
        out_specs=(P("exp", "seq", None), P(None, ("seq", "exp"))),
        check_vma=False,
    )
```
